256 devices in a mesh: pipe: 8 (over y, core), ctx: 32 (over x, z).
Axes of the slice: x: 4, y: 4, z: 8, core: 2. Of those that a mesh axis runs over, the one named last changes fastest.
Arguments:
- queries: bfloat16 [8, 4096, 4096], P('pipe', 'ctx'), may hold values from -240 to 240
- keys: bfloat16 [8, 4096, 4096], P('pipe', 'ctx'), may hold values from -6 to 6
- values: bfloat16 [8, 4096, 4096], P('pipe', 'ctx'), may hold values from -6 to 6
- attn_out: bfloat16 [8, 4096, 4096], P('pipe', 'ctx'), may hold values from -3 to 3
- out_grad: bfloat16 [8, 4096, 4096], P('pipe', 'ctx'), may hold values from -24 to 24
- random_blocks: int32 [8, 32, 64, 3], P('pipe', 'ctx'), may hold values from 0 to 63
- global_blocks: int32 [8, 2], P('pipe'), may hold values from 0 to 63, as said below
- radius: int32 [8, 32], P('pipe', 'ctx'), may hold values from 1 to 2, as said below
Outputs:
- grad_queries: bfloat16 [8, 4096, 4096], P('pipe', 'ctx')
- grad_keys: bfloat16 [8, 4096, 4096], P('pipe', 'ctx')
- grad_values: bfloat16 [8, 4096, 4096], P('pipe', 'ctx')
The draws below stay inside these ranges and needn't reach their ends.
Inputs may be any that keep to these rules, and one draw needn't show every extreme that they name: `global_blocks`: the 2 entries of a section differ. In every section some head has radius 2 and some head has radius 1.
All inputs are finite; a program needn't handle non-finite values.
Results may differ from the reference program's by a relative error of at most 0.0049.
Values may be sent and summed in bfloat16 or wider, within the bound.
No kernel may reach another device: no remote copies, remote signals or barrier semaphores. Data moves between devices by JAX's collectives and lax.ppermute only.
A program may use at most 64 MiB of HBM per device.

```python
import jax
import jax.numpy as jnp
from jax import lax

HD = 128
BLK = 64
RMAX = 2
NG = 2
NR = 3
QG = 8
SECTIONS = 8
HEADS = 32
D = 4096
SEQ = 4096
NB = 64
KB = 10


def base_keys(key):
    return jnp.clip(jax.random.normal(jax.random.fold_in(key, 37), (SECTIONS, SEQ, D), jnp.float32), -6.0, 6.0)


def draw_keys(key, part):
    keys_base = base_keys(key)
    return keys_base.astype(jnp.bfloat16)


def draw_queries(key, part):
    query_base = jnp.clip(jax.random.normal(jax.random.fold_in(key, 41), (SECTIONS, SEQ, D), jnp.float32), -6.0, 6.0)
    return query_base.astype(jnp.bfloat16)


def draw_global_blocks(key, part):
    section_keys = jax.random.split(key, SECTIONS)
    drawn = jax.vmap(lambda section_key: jax.random.permutation(section_key, NB)[:NG])(section_keys).astype(jnp.int32)
    top_section = jax.random.randint(jax.random.fold_in(key, 11), (), 0, SECTIONS)
    low_section = (top_section + 1) % SECTIONS
    top_other = jax.random.randint(jax.random.fold_in(key, 13), (), 0, NB - 1)
    low_other = jax.random.randint(jax.random.fold_in(key, 17), (), 1, NB)
    section_ids = jnp.arange(SECTIONS, dtype=jnp.int32)[:, None]
    column_ids = jnp.arange(NG, dtype=jnp.int32)[None, :]
    top_row = jnp.where(column_ids == 0, NB - 1, top_other)
    low_row = jnp.where(column_ids == 0, 0, low_other)
    drawn = jnp.where(section_ids == top_section, top_row, drawn)
    drawn = jnp.where(section_ids == low_section, low_row, drawn)
    return drawn.astype(jnp.int32)


def draw_radius(key, part):
    drawn = jax.random.randint(jax.random.fold_in(key, 3), (SECTIONS, HEADS), 1, RMAX + 1)
    order = jax.random.permutation(jax.random.fold_in(key, 5), HEADS)
    drawn = drawn.at[:, order[0]].set(RMAX)
    drawn = drawn.at[:, order[1]].set(1)
    return drawn.astype(jnp.int32)


def place_ends(result, key, least, largest):
    index_at = [jax.random.randint(jax.random.fold_in(key, axis), (), 0, length) for axis, length in enumerate(result.shape)]
    longest = result.shape.index(max(result.shape))
    neighbour = index_at[:longest] + [(index_at[longest] + 1) % result.shape[longest]] + index_at[longest + 1:]
    return result.at[tuple(index_at)].set(least).at[tuple(neighbour)].set(largest)


def level_of(own_key, shape, pieces, smallest, largest):
    def one(axis_at, shards_of):
        steps = jax.random.uniform(jax.random.fold_in(jax.random.fold_in(own_key, 6), axis_at), (shards_of,), jnp.float32, smallest / len(pieces), largest / len(pieces))
        return jnp.repeat(jnp.exp(steps), shape[axis_at] // shards_of).reshape((-1,) + (1,) * (len(shape) - axis_at - 1))

    gain = one(*pieces[0])
    for cut in pieces[1:]:
        gain = gain * one(*cut)
    return gain


def bell_draw(key, dims, scale, most, cuts=(), kind=jnp.bfloat16):
    level = level_of(key, dims, cuts, -0.22, 0.18) if cuts else 1.0
    values = jax.random.normal(key, dims, jnp.float32) * scale * level
    return jnp.minimum(jnp.maximum(values, -most), most).astype(kind)


def setup_inputs(seed: int = 0) -> dict:
    seeds = jax.random.split(jax.random.key(seed), 9)
    return {
        "queries": draw_queries(jax.random.fold_in(seeds[8], 71), 0),
        "keys": draw_keys(jax.random.fold_in(seeds[8], 71), 0),
        "values": bell_draw(seeds[2], (SECTIONS, SEQ, D), 1.0, 6.0, ((0, 8), (1, 32))),
        "attn_out": bell_draw(seeds[3], (SECTIONS, SEQ, D), 0.5, 3.0, ((0, 8), (1, 32))),
        "out_grad": bell_draw(seeds[4], (SECTIONS, SEQ, D), 4.0, 24.0, ((0, 8), (1, 32))),
        "random_blocks": place_ends(jax.random.randint(seeds[5], (SECTIONS, HEADS, NB, NR), 0, NB), jax.random.fold_in(seeds[5], 1), 0, NB - 1).astype(jnp.int32),
        "global_blocks": draw_global_blocks(jax.random.fold_in(seeds[8], 71), 0),
        "radius": draw_radius(jax.random.fold_in(seeds[8], 71), 0),
    }


def slot_table(random_list, global_list, head_radius, block_count):
    blocks = jnp.arange(block_count, dtype=jnp.int32)[:, None]
    offsets = jnp.arange(-RMAX, RMAX + 1, dtype=jnp.int32)[None, :]
    window = blocks + offsets
    window_ok = (jnp.abs(offsets) <= head_radius) & (window >= 0) & (window < block_count)
    window = jnp.clip(window, 0, block_count - 1)
    global_slots = jnp.broadcast_to(global_list[None, :], (block_count, global_list.shape[0]))
    global_ok = jnp.abs(global_slots - blocks) > head_radius
    random_ok = jnp.abs(random_list - blocks) > head_radius
    random_ok = random_ok & jnp.all(random_list[:, :, None] != global_list[None, None, :], axis=2)
    earlier = jnp.arange(NR)[None, :] < jnp.arange(NR)[:, None]
    repeated = jnp.any((random_list[:, :, None] == random_list[:, None, :]) & earlier[None], axis=2)
    random_ok = random_ok & jnp.logical_not(repeated)
    slot_index = jnp.concatenate([window, global_slots, random_list], axis=1).astype(jnp.int32)
    slot_valid = jnp.concatenate([window_ok, global_ok, random_ok], axis=1)
    return slot_index, slot_valid


def head_grads(query_rows, key_rows, value_rows, output_rows, grad_rows, random_list, global_list, head_radius):
    block_count = query_rows.shape[0] // BLK
    score_scale = HD ** -0.5
    slot_index, slot_valid = slot_table(random_list, global_list, head_radius, block_count)
    query_blocks = query_rows.reshape(block_count, BLK, HD)
    key_blocks = key_rows.reshape(block_count, BLK, HD)
    value_blocks = value_rows.reshape(block_count, BLK, HD)
    grad_blocks = grad_rows.reshape(block_count, BLK, HD)
    correction = jnp.sum(output_rows.astype(jnp.float32) * grad_rows.astype(jnp.float32), axis=-1).reshape(block_count, BLK)

    def one_group(totals, first_block):
        key_total, value_total = totals
        group_index = lax.dynamic_slice_in_dim(slot_index, first_block, QG, 0)
        group_valid = lax.dynamic_slice_in_dim(slot_valid, first_block, QG, 0)
        group_query = lax.dynamic_slice_in_dim(query_blocks, first_block, QG, 0).astype(jnp.float32)
        group_grad = lax.dynamic_slice_in_dim(grad_blocks, first_block, QG, 0).astype(jnp.float32)
        group_corr = lax.dynamic_slice_in_dim(correction, first_block, QG, 0)
        key_tiles = key_blocks[group_index].reshape(QG, KB * BLK, HD).astype(jnp.float32)
        value_tiles = value_blocks[group_index].reshape(QG, KB * BLK, HD).astype(jnp.float32)
        key_live = jnp.repeat(group_valid, BLK, axis=1)
        scores = jnp.einsum('bid,bjd->bij', group_query, key_tiles) * score_scale
        scores = jnp.where(key_live[:, None, :], scores, -jnp.inf)
        row_max = jnp.max(scores, axis=-1, keepdims=True)
        weights = jnp.exp(scores - row_max)
        attention = weights / jnp.sum(weights, axis=-1, keepdims=True)
        attention_low = lax.optimization_barrier(attention.astype(jnp.bfloat16)).astype(jnp.float32)
        dprobs = jnp.einsum('bid,bjd->bij', group_grad, value_tiles)
        dscores = attention * (dprobs - group_corr[:, :, None])
        dscores_low = lax.optimization_barrier(dscores.astype(jnp.bfloat16)).astype(jnp.float32)
        query_grad = (jnp.einsum('bij,bjd->bid', dscores_low, key_tiles) * score_scale).astype(jnp.bfloat16)
        key_part = jnp.einsum('bij,bid->bjd', dscores_low, group_query).reshape(QG * KB, BLK, HD)
        value_part = jnp.einsum('bij,bid->bjd', attention_low, group_grad).reshape(QG * KB, BLK, HD)
        flat_index = group_index.reshape(-1)
        key_total = key_total.at[flat_index].add(key_part)
        value_total = value_total.at[flat_index].add(value_part)
        return (key_total, value_total), query_grad

    starts = (jnp.arange(block_count // QG) * QG).astype(jnp.int32)
    empty = jnp.zeros((block_count, BLK, HD), jnp.float32)
    (key_total, value_total), query_grad = lax.scan(one_group, (empty, empty), starts)
    query_grad = query_grad.reshape(block_count * BLK, HD)
    key_grad = (key_total * score_scale).astype(jnp.bfloat16).reshape(block_count * BLK, HD)
    value_grad = value_total.astype(jnp.bfloat16).reshape(block_count * BLK, HD)
    return query_grad, key_grad, value_grad


def reference(queries, keys, values, attn_out, out_grad, random_blocks, global_blocks, radius):
    sections, length, model_width = queries.shape
    head_count = model_width // HD
    block_count = length // BLK

    def to_heads_layout(array):
        return array.reshape(sections, length, head_count, HD).transpose(0, 2, 1, 3).reshape(sections * head_count, length, HD)

    def to_section_layout(array):
        joined = array.reshape(sections, head_count, length, HD).transpose(0, 2, 1, 3).reshape(sections, length, model_width)
        return jnp.roll(joined, -1, axis=0)

    problems = (to_heads_layout(queries), to_heads_layout(keys), to_heads_layout(values),
                to_heads_layout(attn_out), to_heads_layout(out_grad),
                random_blocks.reshape(sections * head_count, block_count, NR),
                jnp.repeat(global_blocks, head_count, axis=0),
                radius.reshape(sections * head_count))
    query_grad, key_grad, value_grad = lax.map(lambda problem: head_grads(*problem), problems)
    return to_section_layout(query_grad), to_section_layout(key_grad), to_section_layout(value_grad)
```

```python
import functools

import jax
import jax.numpy as jnp
from jax import lax
from jax.experimental import pallas as pl
from jax.experimental.pallas import tpu as pltpu
from jax.sharding import PartitionSpec as P

HD = 128
BLK = 64
RMAX = 2
NR = 3
KB = 10


def passed_along(value, axis, steps):
    count = lax.axis_size(axis)
    pairs = [(source, (source + steps) % count) for source in range(count)]
    return lax.ppermute(value, axis, pairs)


def slot_table(random_list, global_list, head_radius, block_count):
    blocks = jnp.arange(block_count, dtype=jnp.int32)[:, None]
    offsets = jnp.arange(-RMAX, RMAX + 1, dtype=jnp.int32)[None, :]
    window = blocks + offsets
    window_ok = (jnp.abs(offsets) <= head_radius) & (window >= 0) & (window < block_count)
    window = jnp.clip(window, 0, block_count - 1)
    global_slots = jnp.broadcast_to(global_list[None, :], (block_count, global_list.shape[0]))
    global_ok = jnp.abs(global_slots - blocks) > head_radius
    random_ok = jnp.abs(random_list - blocks) > head_radius
    random_ok = random_ok & jnp.all(random_list[:, :, None] != global_list[None, None, :], axis=2)
    earlier = jnp.arange(NR)[None, :] < jnp.arange(NR)[:, None]
    repeated = jnp.any((random_list[:, :, None] == random_list[:, None, :]) & earlier[None], axis=2)
    random_ok = random_ok & jnp.logical_not(repeated)
    slot_index = jnp.concatenate([window, global_slots, random_list], axis=1)
    slot_valid = jnp.concatenate([window_ok, global_ok, random_ok], axis=1)
    slot_index = jnp.clip(slot_index, 0, block_count - 1)
    return (slot_index.astype(jnp.int32), slot_valid.astype(jnp.int32))


def head_kernel(slot_ref, valid_ref, x_ref, corr_ref, dq_ref, dk_ref, dv_ref,
                kt_ref, vt_ref, dk_acc, dv_acc, *, block_count, chunk_rows):
    score_scale = HD ** (-0.5)
    per_chunk = chunk_rows // BLK
    dk_acc[...] = jnp.zeros_like(dk_acc)
    dv_acc[...] = jnp.zeros_like(dv_acc)
    lane_slot = lax.broadcasted_iota(jnp.int32, (1, KB * BLK), 1) // BLK

    def one_block(i, carry):
        chunk = i // per_chunk
        row = pl.multiple_of((i % per_chunk) * BLK, BLK)
        query = x_ref[chunk, 0, pl.ds(row, BLK), :]
        grad = x_ref[chunk, 3, pl.ds(row, BLK), :]
        live = jnp.zeros((1, KB * BLK), jnp.bool_)
        for j in range(KB):
            kb = slot_ref[i * KB + j]
            kc = kb // per_chunk
            kr = pl.multiple_of((kb % per_chunk) * BLK, BLK)
            kt_ref[pl.ds(j * BLK, BLK), :] = x_ref[kc, 1, pl.ds(kr, BLK), :]
            vt_ref[pl.ds(j * BLK, BLK), :] = x_ref[kc, 2, pl.ds(kr, BLK), :]
            live = live | ((lane_slot == j) & (valid_ref[i * KB + j] != 0))
        key_tiles = kt_ref[...]
        value_tiles = vt_ref[...]
        scores = lax.dot_general(
            query, key_tiles, (((1,), (1,)), ((), ())), preferred_element_type=jnp.float32
        ) * score_scale
        scores = jnp.where(live, scores, -jnp.inf)
        row_max = jnp.max(scores, axis=-1, keepdims=True)
        weights = jnp.exp(scores - row_max)
        attention = weights / jnp.sum(weights, axis=-1, keepdims=True)
        dprobs = lax.dot_general(
            grad, value_tiles, (((1,), (1,)), ((), ())), preferred_element_type=jnp.float32
        )
        corr = corr_ref[pl.ds(pl.multiple_of(i * BLK, BLK), BLK), :]
        dscores = (attention * (dprobs - corr)).astype(jnp.bfloat16)
        query_grad = jnp.dot(dscores, key_tiles, preferred_element_type=jnp.float32) * score_scale
        dq_ref[chunk, pl.ds(row, BLK), :] = query_grad.astype(jnp.bfloat16)
        key_part = lax.dot_general(
            dscores, query, (((0,), (0,)), ((), ())), preferred_element_type=jnp.float32
        )
        value_part = lax.dot_general(
            attention.astype(jnp.bfloat16), grad, (((0,), (0,)), ((), ())),
            preferred_element_type=jnp.float32,
        )
        for j in range(KB):
            kb = slot_ref[i * KB + j]
            dk_acc[kb] = dk_acc[kb] + key_part[j * BLK:(j + 1) * BLK]
            dv_acc[kb] = dv_acc[kb] + value_part[j * BLK:(j + 1) * BLK]
        return carry

    lax.fori_loop(0, block_count, one_block, 0)

    def one_chunk(c, carry):
        for p in range(per_chunk):
            b = c * per_chunk + p
            dk_ref[c, p * BLK:(p + 1) * BLK, :] = (dk_acc[b] * score_scale).astype(jnp.bfloat16)
            dv_ref[c, p * BLK:(p + 1) * BLK, :] = dv_acc[b].astype(jnp.bfloat16)
        return carry

    lax.fori_loop(0, block_count // per_chunk, one_chunk, 0)


def head_grads(x, corr, slot_index, slot_valid, block_count, chunks, chunk_rows):
    vmem = pltpu.MemorySpace.VMEM
    smem = pltpu.MemorySpace.SMEM
    out_shape = jax.ShapeDtypeStruct((chunks, chunk_rows, HD), jnp.bfloat16)
    kernel = functools.partial(head_kernel, block_count=block_count, chunk_rows=chunk_rows)
    return pl.pallas_call(
        kernel,
        out_shape=(out_shape, out_shape, out_shape),
        in_specs=[
            pl.BlockSpec(memory_space=smem),
            pl.BlockSpec(memory_space=smem),
            pl.BlockSpec(memory_space=vmem),
            pl.BlockSpec(memory_space=vmem),
        ],
        out_specs=(
            pl.BlockSpec(memory_space=vmem),
            pl.BlockSpec(memory_space=vmem),
            pl.BlockSpec(memory_space=vmem),
        ),
        scratch_shapes=[
            pltpu.VMEM((KB * BLK, HD), jnp.bfloat16),
            pltpu.VMEM((KB * BLK, HD), jnp.bfloat16),
            pltpu.VMEM((block_count, BLK, HD), jnp.float32),
            pltpu.VMEM((block_count, BLK, HD), jnp.float32),
        ],
        compiler_params=pltpu.CompilerParams(vmem_limit_bytes=48 * 1024 * 1024),
    )(slot_index.reshape(-1), slot_valid.reshape(-1), x, corr)


def body(queries, keys, values, attn_out, out_grad, random_blocks, global_blocks, radius):
    chunks = lax.axis_size("ctx")
    local = queries.shape[1]
    width = queries.shape[2]
    heads = width // HD
    length = local * chunks
    block_count = length // BLK
    correction = jnp.sum(
        (attn_out[0].astype(jnp.float32) * out_grad[0].astype(jnp.float32)).reshape(
            local, heads, HD
        ),
        axis=-1,
    )
    correction = lax.all_to_all(correction.T, "ctx", split_axis=0, concat_axis=0, tiled=True)
    correction = correction.reshape(length, 1)
    stacked = jnp.stack([queries[0], keys[0], values[0], out_grad[0]], axis=0)
    stacked = stacked.reshape(4, local, chunks, HD).transpose(2, 0, 1, 3)
    received = lax.all_to_all(stacked, "ctx", split_axis=0, concat_axis=0, tiled=True)
    slot_index, slot_valid = slot_table(
        random_blocks[0, 0], global_blocks[0], radius[0, 0], block_count
    )
    grads = head_grads(received, correction, slot_index, slot_valid, block_count, chunks, local)
    outs = []
    for g in grads:
        back = lax.all_to_all(g, "ctx", split_axis=0, concat_axis=0, tiled=True)
        back = passed_along(back, "pipe", -1)
        outs.append(back.transpose(1, 0, 2).reshape(1, local, chunks * HD))
    return tuple(outs)


def solution(mesh):
    return jax.shard_map(
        body,
        mesh=mesh,
        in_specs=(
            P("pipe", "ctx", None),
            P("pipe", "ctx", None),
            P("pipe", "ctx", None),
            P("pipe", "ctx", None),
            P("pipe", "ctx", None),
            P("pipe", "ctx", None, None),
            P("pipe", None),
            P("pipe", "ctx"),
        ),
        out_specs=(P("pipe", "ctx", None), P("pipe", "ctx", None), P("pipe", "ctx", None)),
        check_vma=False,
    )
```

```python
import functools

import jax
import jax.numpy as jnp
from jax import lax
from jax.experimental import pallas as pl
from jax.experimental.pallas import tpu as pltpu
from jax.sharding import PartitionSpec as P

HD = 128
BLK = 64
RMAX = 2
NR = 3
KB = 10


def passed_along(value, axis, steps):
    count = lax.axis_size(axis)
    pairs = [(source, (source + steps) % count) for source in range(count)]
    return lax.ppermute(value, axis, pairs)


def slot_table(random_list, global_list, head_radius, block_count):
    blocks = jnp.arange(block_count, dtype=jnp.int32)[:, None]
    offsets = jnp.arange(-RMAX, RMAX + 1, dtype=jnp.int32)[None, :]
    window = blocks + offsets
    window_ok = (jnp.abs(offsets) <= head_radius) & (window >= 0) & (window < block_count)
    window = jnp.clip(window, 0, block_count - 1)
    global_slots = jnp.broadcast_to(global_list[None, :], (block_count, global_list.shape[0]))
    global_ok = jnp.abs(global_slots - blocks) > head_radius
    random_ok = jnp.abs(random_list - blocks) > head_radius
    random_ok = random_ok & jnp.all(random_list[:, :, None] != global_list[None, None, :], axis=2)
    earlier = jnp.arange(NR)[None, :] < jnp.arange(NR)[:, None]
    repeated = jnp.any((random_list[:, :, None] == random_list[:, None, :]) & earlier[None], axis=2)
    random_ok = random_ok & jnp.logical_not(repeated)
    slot_index = jnp.concatenate([window, global_slots, random_list], axis=1)
    slot_valid = jnp.concatenate([window_ok, global_ok, random_ok], axis=1)
    slot_index = jnp.clip(slot_index, 0, block_count - 1)
    return (slot_index.astype(jnp.int32), slot_valid.astype(jnp.int32))


def head_kernel(slot_ref, valid_ref, kv_ref, qd_ref, corr_ref, *rest, block_count,
                chunk_rows, parity, final):
    if final:
        (dk_prev, dv_prev, dq_ref, dk_ref, dv_ref, kt_ref, vt_ref, dk_acc, dv_acc) = rest
    else:
        (dq_ref, dk_acc, dv_acc, kt_ref, vt_ref) = rest
    score_scale = HD ** (-0.5)
    per_chunk = chunk_rows // BLK
    dk_acc[...] = jnp.zeros_like(dk_acc)
    dv_acc[...] = jnp.zeros_like(dv_acc)
    lane_slot = lax.broadcasted_iota(jnp.int32, (1, KB * BLK), 1) // BLK

    def one_block(t, carry):
        i = t * per_chunk + parity
        query = qd_ref[t, 0]
        grad = qd_ref[t, 1]
        live = jnp.zeros((1, KB * BLK), jnp.bool_)
        for j in range(KB):
            kb = slot_ref[i * KB + j]
            kc = kb // per_chunk
            kr = pl.multiple_of((kb % per_chunk) * BLK, BLK)
            kt_ref[pl.ds(j * BLK, BLK), :] = kv_ref[kc, 0, pl.ds(kr, BLK), :]
            vt_ref[pl.ds(j * BLK, BLK), :] = kv_ref[kc, 1, pl.ds(kr, BLK), :]
            live = live | ((lane_slot == j) & (valid_ref[i * KB + j] != 0))
        key_tiles = kt_ref[...]
        value_tiles = vt_ref[...]
        scores = lax.dot_general(
            query, key_tiles, (((1,), (1,)), ((), ())), preferred_element_type=jnp.float32
        ) * score_scale
        scores = jnp.where(live, scores, -jnp.inf)
        row_max = jnp.max(scores, axis=-1, keepdims=True)
        weights = jnp.exp(scores - row_max)
        attention = weights / jnp.sum(weights, axis=-1, keepdims=True)
        dprobs = lax.dot_general(
            grad, value_tiles, (((1,), (1,)), ((), ())), preferred_element_type=jnp.float32
        )
        corr = corr_ref[pl.ds(pl.multiple_of(i * BLK, BLK), BLK), :]
        dscores = (attention * (dprobs - corr)).astype(jnp.bfloat16)
        query_grad = jnp.dot(dscores, key_tiles, preferred_element_type=jnp.float32) * score_scale
        dq_ref[t] = query_grad.astype(jnp.bfloat16)
        key_part = lax.dot_general(
            dscores, query, (((0,), (0,)), ((), ())), preferred_element_type=jnp.float32
        )
        value_part = lax.dot_general(
            attention.astype(jnp.bfloat16), grad, (((0,), (0,)), ((), ())),
            preferred_element_type=jnp.float32,
        )
        for j in range(KB):
            kb = slot_ref[i * KB + j]
            dk_acc[kb] = dk_acc[kb] + key_part[j * BLK:(j + 1) * BLK]
            dv_acc[kb] = dv_acc[kb] + value_part[j * BLK:(j + 1) * BLK]
        return carry

    lax.fori_loop(0, block_count // per_chunk, one_block, 0)

    if final:
        def one_chunk(c, carry):
            for p in range(per_chunk):
                b = c * per_chunk + p
                dk_ref[c, p * BLK:(p + 1) * BLK, :] = (
                    (dk_acc[b] + dk_prev[b]) * score_scale
                ).astype(jnp.bfloat16)
                dv_ref[c, p * BLK:(p + 1) * BLK, :] = (dv_acc[b] + dv_prev[b]).astype(
                    jnp.bfloat16
                )
            return carry

        lax.fori_loop(0, block_count // per_chunk, one_chunk, 0)


def head_part(kv, qd, corr, slot_index, slot_valid, previous, block_count, chunks, chunk_rows,
              parity):
    vmem = pltpu.MemorySpace.VMEM
    smem = pltpu.MemorySpace.SMEM
    final = previous is not None
    dq_shape = jax.ShapeDtypeStruct((chunks, BLK, HD), jnp.bfloat16)
    acc_shape = jax.ShapeDtypeStruct((block_count, BLK, HD), jnp.float32)
    grad_shape = jax.ShapeDtypeStruct((chunks, chunk_rows, HD), jnp.bfloat16)
    kernel = functools.partial(
        head_kernel, block_count=block_count, chunk_rows=chunk_rows, parity=parity, final=final
    )
    operands = [slot_index.reshape(-1), slot_valid.reshape(-1), kv, qd, corr]
    scratch = [pltpu.VMEM((KB * BLK, HD), jnp.bfloat16), pltpu.VMEM((KB * BLK, HD), jnp.bfloat16)]
    if final:
        operands += list(previous)
        out_shape = (dq_shape, grad_shape, grad_shape)
        scratch += [pltpu.VMEM((block_count, BLK, HD), jnp.float32)] * 2
    else:
        out_shape = (dq_shape, acc_shape, acc_shape)
    in_specs = [pl.BlockSpec(memory_space=smem)] * 2 + [pl.BlockSpec(memory_space=vmem)] * (
        len(operands) - 2
    )
    return pl.pallas_call(
        kernel,
        out_shape=out_shape,
        in_specs=in_specs,
        out_specs=tuple(pl.BlockSpec(memory_space=vmem) for _ in out_shape),
        scratch_shapes=scratch,
        compiler_params=pltpu.CompilerParams(vmem_limit_bytes=48 * 1024 * 1024),
    )(*operands)


def to_chunks(rows, chunks):
    count, local, width = rows.shape
    return rows.reshape(count, local, chunks, width // chunks).transpose(2, 0, 1, 3)


def body(queries, keys, values, attn_out, out_grad, random_blocks, global_blocks, radius):
    chunks = lax.axis_size("ctx")
    local = queries.shape[1]
    width = queries.shape[2]
    heads = width // HD
    length = local * chunks
    block_count = length // BLK
    per_chunk = local // BLK
    correction = jnp.sum(
        (attn_out[0].astype(jnp.float32) * out_grad[0].astype(jnp.float32)).reshape(
            local, heads, HD
        ),
        axis=-1,
    )
    correction = lax.all_to_all(correction.T, "ctx", split_axis=0, concat_axis=0, tiled=True)
    correction = correction.reshape(length, 1)
    kv = to_chunks(jnp.stack([keys[0], values[0]], axis=0), chunks)
    kv = lax.all_to_all(kv, "ctx", split_axis=0, concat_axis=0, tiled=True)
    slot_index, slot_valid = slot_table(
        random_blocks[0, 0], global_blocks[0], radius[0, 0], block_count
    )
    previous = None
    after = kv
    dq_parts = []
    returned = []
    for parity in range(per_chunk):
        rows = slice(parity * BLK, (parity + 1) * BLK)
        qd = to_chunks(jnp.stack([queries[0, rows], out_grad[0, rows]], axis=0), chunks)
        qd, _ = lax.optimization_barrier((qd, after))
        qd = lax.all_to_all(qd, "ctx", split_axis=0, concat_axis=0, tiled=True)
        after = qd
        dq, dk, dv = head_part(
            kv, qd, correction, slot_index, slot_valid, previous, block_count, chunks, local,
            parity,
        )
        previous = (dk, dv)
        back = lax.all_to_all(dq, "ctx", split_axis=0, concat_axis=0, tiled=True)
        dq_parts.append(passed_along(back, "pipe", -1))
    for g in previous:
        back = lax.all_to_all(g, "ctx", split_axis=0, concat_axis=0, tiled=True)
        returned.append(passed_along(back, "pipe", -1))
    dq_all = jnp.concatenate(dq_parts, axis=1)
    outs = [dq_all] + returned
    return tuple(o.transpose(1, 0, 2).reshape(1, local, chunks * HD) for o in outs)


def solution(mesh):
    return jax.shard_map(
        body,
        mesh=mesh,
        in_specs=(
            P("pipe", "ctx", None),
            P("pipe", "ctx", None),
            P("pipe", "ctx", None),
            P("pipe", "ctx", None),
            P("pipe", "ctx", None),
            P("pipe", "ctx", None, None),
            P("pipe", None),
            P("pipe", "ctx"),
        ),
        out_specs=(P("pipe", "ctx", None), P("pipe", "ctx", None), P("pipe", "ctx", None)),
        check_vma=False,
    )
```

```python
import functools

import jax
import jax.numpy as jnp
from jax import lax
from jax.experimental import pallas as pl
from jax.experimental.pallas import tpu as pltpu
from jax.sharding import PartitionSpec as P

HD = 128
BLK = 64
RMAX = 2
NR = 3
KB = 10


def passed_along(value, axis, steps):
    count = lax.axis_size(axis)
    pairs = [(source, (source + steps) % count) for source in range(count)]
    return lax.ppermute(value, axis, pairs)


def slot_table(random_list, global_list, head_radius, block_count):
    blocks = jnp.arange(block_count, dtype=jnp.int32)[:, None]
    offsets = jnp.arange(-RMAX, RMAX + 1, dtype=jnp.int32)[None, :]
    window = blocks + offsets
    window_ok = (jnp.abs(offsets) <= head_radius) & (window >= 0) & (window < block_count)
    window = jnp.clip(window, 0, block_count - 1)
    global_slots = jnp.broadcast_to(global_list[None, :], (block_count, global_list.shape[0]))
    global_ok = jnp.abs(global_slots - blocks) > head_radius
    random_ok = jnp.abs(random_list - blocks) > head_radius
    random_ok = random_ok & jnp.all(random_list[:, :, None] != global_list[None, None, :], axis=2)
    earlier = jnp.arange(NR)[None, :] < jnp.arange(NR)[:, None]
    repeated = jnp.any((random_list[:, :, None] == random_list[:, None, :]) & earlier[None], axis=2)
    random_ok = random_ok & jnp.logical_not(repeated)
    slot_index = jnp.concatenate([window, global_slots, random_list], axis=1)
    slot_valid = jnp.concatenate([window_ok, global_ok, random_ok], axis=1)
    slot_index = jnp.clip(slot_index, 0, block_count - 1)
    return (slot_index.astype(jnp.int32), slot_valid.astype(jnp.int32))


def head_kernel(slot_ref, valid_ref, kv_ref, qd_ref, corr_ref, *rest, block_count,
                chunk_rows, parity, final):
    if final:
        (dq_prev, dk_prev, dv_prev, out_ref, kt_ref, vt_ref, dk_acc, dv_acc) = rest
        out_ref[:, 0:parity * BLK, :] = dq_prev[...]
        dq_ref = out_ref.at[:, parity * BLK:(parity + 1) * BLK, :]
        dk_ref = out_ref.at[:, chunk_rows:2 * chunk_rows, :]
        dv_ref = out_ref.at[:, 2 * chunk_rows:3 * chunk_rows, :]
    else:
        (dq_ref, dk_acc, dv_acc, kt_ref, vt_ref) = rest
    score_scale = HD ** (-0.5)
    per_chunk = chunk_rows // BLK
    dk_acc[...] = jnp.zeros_like(dk_acc)
    dv_acc[...] = jnp.zeros_like(dv_acc)
    lane_slot = lax.broadcasted_iota(jnp.int32, (1, KB * BLK), 1) // BLK

    def one_block(t, carry):
        i = t * per_chunk + parity
        query = qd_ref[t, 0]
        grad = qd_ref[t, 1]
        live = jnp.zeros((1, KB * BLK), jnp.bool_)
        for j in range(KB):
            kb = slot_ref[i * KB + j]
            kc = kb // per_chunk
            kr = pl.multiple_of((kb % per_chunk) * BLK, BLK)
            kt_ref[pl.ds(j * BLK, BLK), :] = kv_ref[kc, pl.ds(kr, BLK), :]
            vt_ref[pl.ds(j * BLK, BLK), :] = kv_ref[kc, pl.ds(chunk_rows + kr, BLK), :]
            live = live | ((lane_slot == j) & (valid_ref[i * KB + j] != 0))
        key_tiles = kt_ref[...]
        value_tiles = vt_ref[...]
        scores = lax.dot_general(
            query, key_tiles, (((1,), (1,)), ((), ())), preferred_element_type=jnp.float32
        ) * score_scale
        scores = jnp.where(live, scores, -jnp.inf)
        row_max = jnp.max(scores, axis=-1, keepdims=True)
        weights = jnp.exp(scores - row_max)
        attention = weights / jnp.sum(weights, axis=-1, keepdims=True)
        dprobs = lax.dot_general(
            grad, value_tiles, (((1,), (1,)), ((), ())), preferred_element_type=jnp.float32
        )
        corr = corr_ref[pl.ds(pl.multiple_of(i * BLK, BLK), BLK), :]
        dscores = (attention * (dprobs - corr)).astype(jnp.bfloat16)
        query_grad = jnp.dot(dscores, key_tiles, preferred_element_type=jnp.float32) * score_scale
        dq_ref[t] = query_grad.astype(jnp.bfloat16)
        key_part = lax.dot_general(
            dscores, query, (((0,), (0,)), ((), ())), preferred_element_type=jnp.float32
        )
        value_part = lax.dot_general(
            attention.astype(jnp.bfloat16), grad, (((0,), (0,)), ((), ())),
            preferred_element_type=jnp.float32,
        )
        for j in range(KB):
            kb = slot_ref[i * KB + j]
            dk_acc[kb] = dk_acc[kb] + key_part[j * BLK:(j + 1) * BLK]
            dv_acc[kb] = dv_acc[kb] + value_part[j * BLK:(j + 1) * BLK]
        return carry

    lax.fori_loop(0, block_count // per_chunk, one_block, 0)

    if final:
        def one_chunk(c, carry):
            for p in range(per_chunk):
                b = c * per_chunk + p
                dk_ref[c, p * BLK:(p + 1) * BLK, :] = (
                    (dk_acc[b] + dk_prev[b]) * score_scale
                ).astype(jnp.bfloat16)
                dv_ref[c, p * BLK:(p + 1) * BLK, :] = (dv_acc[b] + dv_prev[b]).astype(
                    jnp.bfloat16
                )
            return carry

        lax.fori_loop(0, block_count // per_chunk, one_chunk, 0)


def head_part(kv, qd, corr, slot_index, slot_valid, previous, block_count, chunks, chunk_rows,
              parity):
    vmem = pltpu.MemorySpace.VMEM
    smem = pltpu.MemorySpace.SMEM
    final = previous is not None
    dq_shape = jax.ShapeDtypeStruct((chunks, BLK, HD), jnp.bfloat16)
    acc_shape = jax.ShapeDtypeStruct((block_count, BLK, HD), jnp.float32)
    kernel = functools.partial(
        head_kernel, block_count=block_count, chunk_rows=chunk_rows, parity=parity, final=final
    )
    operands = [slot_index.reshape(-1), slot_valid.reshape(-1), kv, qd, corr]
    scratch = [pltpu.VMEM((KB * BLK, HD), jnp.bfloat16), pltpu.VMEM((KB * BLK, HD), jnp.bfloat16)]
    if final:
        operands += list(previous)
        out_shape = (jax.ShapeDtypeStruct((chunks, 3 * chunk_rows, HD), jnp.bfloat16),)
        scratch += [pltpu.VMEM((block_count, BLK, HD), jnp.float32)] * 2
    else:
        out_shape = (dq_shape, acc_shape, acc_shape)
    in_specs = [pl.BlockSpec(memory_space=smem)] * 2 + [pl.BlockSpec(memory_space=vmem)] * (
        len(operands) - 2
    )
    return pl.pallas_call(
        kernel,
        out_shape=out_shape,
        in_specs=in_specs,
        out_specs=tuple(pl.BlockSpec(memory_space=vmem) for _ in out_shape),
        scratch_shapes=scratch,
        compiler_params=pltpu.CompilerParams(vmem_limit_bytes=48 * 1024 * 1024),
    )(*operands)


def to_chunks(rows, chunks):
    count, local, width = rows.shape
    return rows.reshape(count, local, chunks, width // chunks).transpose(2, 0, 1, 3)


def split_pieces(value, count):
    pieces = []
    rest = value
    for _ in range(count):
        piece = lax.optimization_barrier(rest.astype(jnp.bfloat16))
        pieces.append(piece)
        rest = rest - piece.astype(jnp.float32)
    return pieces


def body(queries, keys, values, attn_out, out_grad, random_blocks, global_blocks, radius):
    chunks = lax.axis_size("ctx")
    local = queries.shape[1]
    width = queries.shape[2]
    heads = width // HD
    length = local * chunks
    block_count = length // BLK
    per_chunk = local // BLK
    correction = jnp.sum(
        (attn_out[0].astype(jnp.float32) * out_grad[0].astype(jnp.float32)).reshape(
            local, heads, HD
        ),
        axis=-1,
    )
    pieces = jnp.stack(split_pieces(correction.T, 3), axis=1)
    pieces = jnp.pad(pieces, ((0, 0), (0, 8 - pieces.shape[1]), (0, 0)))
    kv = to_chunks(jnp.stack([keys[0], values[0]], axis=0), chunks).reshape(chunks, 2 * local, HD)
    kv = jnp.concatenate([kv, pieces], axis=1)
    kv = lax.all_to_all(kv, "ctx", split_axis=0, concat_axis=0, tiled=True)
    got = kv[:, 2 * local:2 * local + 3, :].astype(jnp.float32)
    correction = ((got[:, 0] + got[:, 1]) + got[:, 2]).reshape(length, 1)
    slot_index, slot_valid = slot_table(
        random_blocks[0, 0], global_blocks[0], radius[0, 0], block_count
    )
    previous = None
    after = kv
    for parity in range(per_chunk):
        rows = slice(parity * BLK, (parity + 1) * BLK)
        qd = to_chunks(jnp.stack([queries[0, rows], out_grad[0, rows]], axis=0), chunks)
        qd, _ = lax.optimization_barrier((qd, after))
        qd = lax.all_to_all(qd, "ctx", split_axis=0, concat_axis=0, tiled=True)
        after = qd
        result = head_part(
            kv, qd, correction, slot_index, slot_valid, previous, block_count, chunks, local,
            parity,
        )
        previous = result
    back = lax.all_to_all(result[0], "ctx", split_axis=0, concat_axis=0, tiled=True)
    back = passed_along(back, "pipe", -1)
    outs = [back[:, k * local:(k + 1) * local] for k in range(3)]
    return tuple(o.transpose(1, 0, 2).reshape(1, local, chunks * HD) for o in outs)


def solution(mesh):
    return jax.shard_map(
        body,
        mesh=mesh,
        in_specs=(
            P("pipe", "ctx", None),
            P("pipe", "ctx", None),
            P("pipe", "ctx", None),
            P("pipe", "ctx", None),
            P("pipe", "ctx", None),
            P("pipe", "ctx", None, None),
            P("pipe", None),
            P("pipe", "ctx"),
        ),
        out_specs=(P("pipe", "ctx", None), P("pipe", "ctx", None), P("pipe", "ctx", None)),
        check_vma=False,
    )
```

```python
import functools

import jax
import jax.numpy as jnp
from jax import lax
from jax.experimental import pallas as pl
from jax.experimental.pallas import tpu as pltpu
from jax.sharding import PartitionSpec as P


HD = 128
BLK = 64
RMAX = 2
NR = 3
KB = 10


def passed_along(value, axis, steps):
    count = lax.axis_size(axis)
    pairs = [(source, (source + steps) % count) for source in range(count)]
    return lax.ppermute(value, axis, pairs)


def slot_table(random_list, global_list, head_radius, block_count):
    blocks = jnp.arange(block_count, dtype=jnp.int32)[:, None]
    offsets = jnp.arange(-RMAX, RMAX + 1, dtype=jnp.int32)[None, :]
    window = blocks + offsets
    window_ok = (jnp.abs(offsets) <= head_radius) & (window >= 0) & (window < block_count)
    window = jnp.clip(window, 0, block_count - 1)
    global_slots = jnp.broadcast_to(global_list[None, :], (block_count, global_list.shape[0]))
    global_ok = jnp.abs(global_slots - blocks) > head_radius
    random_ok = jnp.abs(random_list - blocks) > head_radius
    random_ok = random_ok & jnp.all(random_list[:, :, None] != global_list[None, None, :], axis=2)
    earlier = jnp.arange(NR)[None, :] < jnp.arange(NR)[:, None]
    repeated = jnp.any((random_list[:, :, None] == random_list[:, None, :]) & earlier[None], axis=2)
    random_ok = random_ok & jnp.logical_not(repeated)
    slot_index = jnp.concatenate([window, global_slots, random_list], axis=1)
    slot_valid = jnp.concatenate([window_ok, global_ok, random_ok], axis=1)
    slot_index = jnp.clip(slot_index, 0, block_count - 1)
    return (slot_index.astype(jnp.int32), slot_valid.astype(jnp.int32))


def head_kernel(slot_ref, valid_ref, kv_ref, qd_ref, corr_ref, *rest, block_count,
                chunk_rows, parity, final):
    if final:
        (dq_prev, dk_prev, dv_prev, out_ref, kt_ref, vt_ref, dk_acc, dv_acc) = rest
        out_ref[:, 0:parity * BLK, :] = dq_prev[...]
        dq_ref = out_ref.at[:, parity * BLK:(parity + 1) * BLK, :]
        dk_ref = out_ref.at[:, chunk_rows:2 * chunk_rows, :]
        dv_ref = out_ref.at[:, 2 * chunk_rows:3 * chunk_rows, :]
    else:
        (dq_ref, dk_acc, dv_acc, kt_ref, vt_ref) = rest
    score_scale = HD ** (-0.5)
    per_chunk = chunk_rows // BLK
    dk_acc[...] = jnp.zeros_like(dk_acc)
    dv_acc[...] = jnp.zeros_like(dv_acc)
    lane_slot = lax.broadcasted_iota(jnp.int32, (1, KB * BLK), 1) // BLK

    def one_block(t, carry):
        i = t * per_chunk + parity
        query = qd_ref[t, 0]
        grad = qd_ref[t, 1]
        live = jnp.zeros((1, KB * BLK), jnp.bool_)
        for j in range(KB):
            kb = slot_ref[i * KB + j]
            kc = kb // per_chunk
            kr = pl.multiple_of((kb % per_chunk) * BLK, BLK)
            kt_ref[pl.ds(j * BLK, BLK), :] = kv_ref[kc, pl.ds(kr, BLK), :]
            vt_ref[pl.ds(j * BLK, BLK), :] = kv_ref[kc, pl.ds(chunk_rows + kr, BLK), :]
            live = live | ((lane_slot == j) & (valid_ref[i * KB + j] != 0))
        key_tiles = kt_ref[...]
        value_tiles = vt_ref[...]
        scores = lax.dot_general(
            query, key_tiles, (((1,), (1,)), ((), ())), preferred_element_type=jnp.float32
        ) * score_scale
        scores = jnp.where(live, scores, -jnp.inf)
        row_max = jnp.max(scores, axis=-1, keepdims=True)
        weights = jnp.exp(scores - row_max)
        attention = weights / jnp.sum(weights, axis=-1, keepdims=True)
        dprobs = lax.dot_general(
            grad, value_tiles, (((1,), (1,)), ((), ())), preferred_element_type=jnp.float32
        )
        corr = corr_ref[pl.ds(pl.multiple_of(i * BLK, BLK), BLK), :]
        dscores = (attention * (dprobs - corr)).astype(jnp.bfloat16)
        query_grad = jnp.dot(dscores, key_tiles, preferred_element_type=jnp.float32) * score_scale
        dq_ref[t] = query_grad.astype(jnp.bfloat16)
        key_part = lax.dot_general(
            dscores, query, (((0,), (0,)), ((), ())), preferred_element_type=jnp.float32
        )
        value_part = lax.dot_general(
            attention.astype(jnp.bfloat16), grad, (((0,), (0,)), ((), ())),
            preferred_element_type=jnp.float32,
        )
        for j in range(KB):
            kb = slot_ref[i * KB + j]
            dk_acc[kb] = dk_acc[kb] + key_part[j * BLK:(j + 1) * BLK]
            dv_acc[kb] = dv_acc[kb] + value_part[j * BLK:(j + 1) * BLK]
        return carry

    lax.fori_loop(0, block_count // per_chunk, one_block, 0)

    if final:
        def one_chunk(c, carry):
            for p in range(per_chunk):
                b = c * per_chunk + p
                dk_ref[c, p * BLK:(p + 1) * BLK, :] = (
                    (dk_acc[b] + dk_prev[b]) * score_scale
                ).astype(jnp.bfloat16)
                dv_ref[c, p * BLK:(p + 1) * BLK, :] = (dv_acc[b] + dv_prev[b]).astype(
                    jnp.bfloat16
                )
            return carry

        lax.fori_loop(0, block_count // per_chunk, one_chunk, 0)


def head_part(kv, qd, corr, slot_index, slot_valid, previous, block_count, chunks, chunk_rows,
              parity):
    vmem = pltpu.MemorySpace.VMEM
    smem = pltpu.MemorySpace.SMEM
    final = previous is not None
    dq_shape = jax.ShapeDtypeStruct((chunks, BLK, HD), jnp.bfloat16)
    acc_shape = jax.ShapeDtypeStruct((block_count, BLK, HD), jnp.float32)
    kernel = functools.partial(
        head_kernel, block_count=block_count, chunk_rows=chunk_rows, parity=parity, final=final
    )
    operands = [slot_index.reshape(-1), slot_valid.reshape(-1), kv, qd, corr]
    scratch = [pltpu.VMEM((KB * BLK, HD), jnp.bfloat16), pltpu.VMEM((KB * BLK, HD), jnp.bfloat16)]
    if final:
        operands += list(previous)
        out_shape = (jax.ShapeDtypeStruct((chunks, 3 * chunk_rows, HD), jnp.bfloat16),)
        scratch += [pltpu.VMEM((block_count, BLK, HD), jnp.float32)] * 2
    else:
        out_shape = (dq_shape, acc_shape, acc_shape)
    in_specs = [pl.BlockSpec(memory_space=smem)] * 2 + [pl.BlockSpec(memory_space=vmem)] * (
        len(operands) - 2
    )
    return pl.pallas_call(
        kernel,
        out_shape=out_shape,
        in_specs=in_specs,
        out_specs=tuple(pl.BlockSpec(memory_space=vmem) for _ in out_shape),
        scratch_shapes=scratch,
        compiler_params=pltpu.CompilerParams(vmem_limit_bytes=48 * 1024 * 1024),
    )(*operands)


def to_chunks(rows, chunks):
    count, local, width = rows.shape
    return rows.reshape(count, local, chunks, width // chunks).transpose(2, 0, 1, 3)


def split_pieces(value, count):
    pieces = []
    rest = value
    for _ in range(count):
        piece = lax.optimization_barrier(rest.astype(jnp.bfloat16))
        pieces.append(piece)
        rest = rest - piece.astype(jnp.float32)
    return pieces


def body(queries, keys, values, attn_out, out_grad, random_blocks, global_blocks, radius):
    chunks = lax.axis_size("ctx")
    local = queries.shape[1]
    width = queries.shape[2]
    heads = width // HD
    length = local * chunks
    block_count = length // BLK
    per_chunk = local // BLK
    correction = jnp.sum(
        (attn_out[0].astype(jnp.float32) * out_grad[0].astype(jnp.float32)).reshape(
            local, heads, HD
        ),
        axis=-1,
    )
    pieces = jnp.stack(split_pieces(correction.T, 3), axis=1)
    pieces = jnp.pad(pieces, ((0, 0), (0, 8 - pieces.shape[1]), (0, 0)))
    kv = to_chunks(jnp.stack([keys[0], values[0]], axis=0), chunks).reshape(chunks, 2 * local, HD)
    kv = jnp.concatenate([kv, pieces], axis=1)
    kv = lax.all_to_all(kv, "ctx", split_axis=0, concat_axis=0, tiled=True)
    after = kv
    kv = passed_along(kv, "pipe", -1)
    got = kv[:, 2 * local:2 * local + 3, :].astype(jnp.float32)
    correction = ((got[:, 0] + got[:, 1]) + got[:, 2]).reshape(length, 1)
    random_list = passed_along(random_blocks[0, 0], "pipe", -1)
    global_list = passed_along(global_blocks[0], "pipe", -1)
    head_radius = passed_along(radius[0, 0], "pipe", -1)
    slot_index, slot_valid = slot_table(random_list, global_list, head_radius, block_count)
    previous = None
    for parity in range(per_chunk):
        rows = slice(parity * BLK, (parity + 1) * BLK)
        qd = to_chunks(jnp.stack([queries[0, rows], out_grad[0, rows]], axis=0), chunks)
        qd, _ = lax.optimization_barrier((qd, after))
        qd = lax.all_to_all(qd, "ctx", split_axis=0, concat_axis=0, tiled=True)
        after = qd
        qd = passed_along(qd, "pipe", -1)
        result = head_part(
            kv, qd, correction, slot_index, slot_valid, previous, block_count, chunks, local,
            parity,
        )
        previous = result
    back = lax.all_to_all(result[0], "ctx", split_axis=0, concat_axis=0, tiled=True)
    outs = [back[:, k * local:(k + 1) * local] for k in range(3)]
    return tuple(o.transpose(1, 0, 2).reshape(1, local, chunks * HD) for o in outs)


def solution(mesh):
    return jax.shard_map(
        body,
        mesh=mesh,
        in_specs=(
            P("pipe", "ctx", None),
            P("pipe", "ctx", None),
            P("pipe", "ctx", None),
            P("pipe", "ctx", None),
            P("pipe", "ctx", None),
            P("pipe", "ctx", None, None),
            P("pipe", None),
            P("pipe", "ctx"),
        ),
        out_specs=(P("pipe", "ctx", None), P("pipe", "ctx", None), P("pipe", "ctx", None)),
        check_vma=False,
    )
```

```python
import functools

import jax
import jax.numpy as jnp
from jax import lax
from jax.experimental import pallas as pl
from jax.experimental.pallas import tpu as pltpu
from jax.sharding import PartitionSpec as P


HD = 128
BLK = 64
RMAX = 2
NR = 3
KB = 10


def passed_along(value, axis, steps):
    count = lax.axis_size(axis)
    pairs = [(source, (source + steps) % count) for source in range(count)]
    return lax.ppermute(value, axis, pairs)


def slot_table(random_list, global_list, head_radius, block_count):
    blocks = jnp.arange(block_count, dtype=jnp.int32)[:, None]
    offsets = jnp.arange(-RMAX, RMAX + 1, dtype=jnp.int32)[None, :]
    window = blocks + offsets
    window_ok = (jnp.abs(offsets) <= head_radius) & (window >= 0) & (window < block_count)
    window = jnp.clip(window, 0, block_count - 1)
    global_slots = jnp.broadcast_to(global_list[None, :], (block_count, global_list.shape[0]))
    global_ok = jnp.abs(global_slots - blocks) > head_radius
    random_ok = jnp.abs(random_list - blocks) > head_radius
    random_ok = random_ok & jnp.all(random_list[:, :, None] != global_list[None, None, :], axis=2)
    earlier = jnp.arange(NR)[None, :] < jnp.arange(NR)[:, None]
    repeated = jnp.any((random_list[:, :, None] == random_list[:, None, :]) & earlier[None], axis=2)
    random_ok = random_ok & jnp.logical_not(repeated)
    slot_index = jnp.concatenate([window, global_slots, random_list], axis=1)
    slot_valid = jnp.concatenate([window_ok, global_ok, random_ok], axis=1)
    slot_index = jnp.clip(slot_index, 0, block_count - 1)
    return (slot_index.astype(jnp.int32), slot_valid.astype(jnp.int32))


def head_kernel(slot_ref, valid_ref, kv_ref, qd_ref, corr_ref, *rest, block_count,
                chunk_rows, parity, final):
    if final:
        (dq_prev, dk_prev, dv_prev, out_ref, kt_ref, vt_ref, dk_acc, dv_acc) = rest
        out_ref[:, 0:parity * BLK, :] = dq_prev[...]
        dq_ref = out_ref.at[:, parity * BLK:(parity + 1) * BLK, :]
        dk_ref = out_ref.at[:, chunk_rows:2 * chunk_rows, :]
        dv_ref = out_ref.at[:, 2 * chunk_rows:3 * chunk_rows, :]
    else:
        (dq_ref, dk_acc, dv_acc, kt_ref, vt_ref) = rest
    score_scale = HD ** (-0.5)
    per_chunk = chunk_rows // BLK
    dk_acc[...] = jnp.zeros_like(dk_acc)
    dv_acc[...] = jnp.zeros_like(dv_acc)
    lane_slot = lax.broadcasted_iota(jnp.int32, (1, KB * BLK), 1) // BLK

    def one_block(t, carry):
        i = t * per_chunk + parity
        query = qd_ref[t, 0]
        grad = qd_ref[t, 1]
        live = jnp.zeros((1, KB * BLK), jnp.bool_)
        for j in range(KB):
            kb = slot_ref[i * KB + j]
            kc = kb // per_chunk
            kr = pl.multiple_of((kb % per_chunk) * BLK, BLK)
            kt_ref[pl.ds(j * BLK, BLK), :] = kv_ref[kc, pl.ds(kr, BLK), :]
            vt_ref[pl.ds(j * BLK, BLK), :] = kv_ref[kc, pl.ds(chunk_rows + kr, BLK), :]
            live = live | ((lane_slot == j) & (valid_ref[i * KB + j] != 0))
        key_tiles = kt_ref[...]
        value_tiles = vt_ref[...]
        scores = lax.dot_general(
            query, key_tiles, (((1,), (1,)), ((), ())), preferred_element_type=jnp.float32
        ) * score_scale
        scores = jnp.where(live, scores, -jnp.inf)
        row_max = jnp.max(scores, axis=-1, keepdims=True)
        weights = jnp.exp(scores - row_max)
        attention = weights / jnp.sum(weights, axis=-1, keepdims=True)
        dprobs = lax.dot_general(
            grad, value_tiles, (((1,), (1,)), ((), ())), preferred_element_type=jnp.float32
        )
        corr = corr_ref[pl.ds(pl.multiple_of(i * BLK, BLK), BLK), :]
        dscores = (attention * (dprobs - corr)).astype(jnp.bfloat16)
        query_grad = jnp.dot(dscores, key_tiles, preferred_element_type=jnp.float32) * score_scale
        dq_ref[t] = query_grad.astype(jnp.bfloat16)
        key_part = lax.dot_general(
            dscores, query, (((0,), (0,)), ((), ())), preferred_element_type=jnp.float32
        )
        value_part = lax.dot_general(
            attention.astype(jnp.bfloat16), grad, (((0,), (0,)), ((), ())),
            preferred_element_type=jnp.float32,
        )
        for j in range(KB):
            kb = slot_ref[i * KB + j]
            dk_acc[kb] = dk_acc[kb] + key_part[j * BLK:(j + 1) * BLK]
            dv_acc[kb] = dv_acc[kb] + value_part[j * BLK:(j + 1) * BLK]
        return carry

    lax.fori_loop(0, block_count // per_chunk, one_block, 0)

    if final:
        def one_chunk(c, carry):
            for p in range(per_chunk):
                b = c * per_chunk + p
                dk_ref[c, p * BLK:(p + 1) * BLK, :] = (
                    (dk_acc[b] + dk_prev[b]) * score_scale
                ).astype(jnp.bfloat16)
                dv_ref[c, p * BLK:(p + 1) * BLK, :] = (dv_acc[b] + dv_prev[b]).astype(
                    jnp.bfloat16
                )
            return carry

        lax.fori_loop(0, block_count // per_chunk, one_chunk, 0)


def head_part(kv, qd, corr, slot_index, slot_valid, previous, block_count, chunks, chunk_rows,
              parity):
    vmem = pltpu.MemorySpace.VMEM
    smem = pltpu.MemorySpace.SMEM
    final = previous is not None
    dq_shape = jax.ShapeDtypeStruct((chunks, BLK, HD), jnp.bfloat16)
    acc_shape = jax.ShapeDtypeStruct((block_count, BLK, HD), jnp.float32)
    kernel = functools.partial(
        head_kernel, block_count=block_count, chunk_rows=chunk_rows, parity=parity, final=final
    )
    operands = [slot_index.reshape(-1), slot_valid.reshape(-1), kv, qd, corr]
    scratch = [pltpu.VMEM((KB * BLK, HD), jnp.bfloat16), pltpu.VMEM((KB * BLK, HD), jnp.bfloat16)]
    if final:
        operands += list(previous)
        out_shape = (jax.ShapeDtypeStruct((chunks, 3 * chunk_rows, HD), jnp.bfloat16),)
        scratch += [pltpu.VMEM((block_count, BLK, HD), jnp.float32)] * 2
    else:
        out_shape = (dq_shape, acc_shape, acc_shape)
    in_specs = [pl.BlockSpec(memory_space=smem)] * 2 + [pl.BlockSpec(memory_space=vmem)] * (
        len(operands) - 2
    )
    return pl.pallas_call(
        kernel,
        out_shape=out_shape,
        in_specs=in_specs,
        out_specs=tuple(pl.BlockSpec(memory_space=vmem) for _ in out_shape),
        scratch_shapes=scratch,
        compiler_params=pltpu.CompilerParams(vmem_limit_bytes=48 * 1024 * 1024),
    )(*operands)


def to_chunks(rows, chunks):
    count, local, width = rows.shape
    return rows.reshape(count, local, chunks, width // chunks).transpose(2, 0, 1, 3)


def split_pieces(value, count):
    pieces = []
    rest = value
    for _ in range(count):
        piece = lax.optimization_barrier(rest.astype(jnp.bfloat16))
        pieces.append(piece)
        rest = rest - piece.astype(jnp.float32)
    return pieces


def body(queries, keys, values, attn_out, out_grad, random_blocks, global_blocks, radius):
    chunks = lax.axis_size("ctx")
    local = queries.shape[1]
    width = queries.shape[2]
    heads = width // HD
    length = local * chunks
    block_count = length // BLK
    per_chunk = local // BLK
    ints = jnp.concatenate(
        [random_blocks.reshape(-1), global_blocks.reshape(-1), radius.reshape(-1)]
    )
    ints = passed_along(ints, "pipe", -1)
    random_list = ints[:block_count * NR].reshape(block_count, NR)
    global_list = ints[block_count * NR:-1]
    head_radius = ints[-1]
    shipped = []
    for parity in range(per_chunk):
        rows = slice(parity * BLK, (parity + 1) * BLK)
        qd = to_chunks(jnp.stack([queries[0, rows], out_grad[0, rows]], axis=0), chunks)
        qd, _ = lax.optimization_barrier((qd, ints))
        shipped.append(passed_along(qd, "pipe", -1))
    correction = jnp.sum(
        (attn_out[0].astype(jnp.float32) * out_grad[0].astype(jnp.float32)).reshape(
            local, heads, HD
        ),
        axis=-1,
    )
    pieces = jnp.stack(split_pieces(correction.T, 3), axis=1)
    pieces = jnp.pad(pieces, ((0, 0), (0, 8 - pieces.shape[1]), (0, 0)))
    kv = to_chunks(jnp.stack([keys[0], values[0]], axis=0), chunks).reshape(chunks, 2 * local, HD)
    kv = jnp.concatenate([kv, pieces], axis=1)
    kv = lax.all_to_all(kv, "ctx", split_axis=0, concat_axis=0, tiled=True)
    after = kv
    kv, _ = lax.optimization_barrier((kv, shipped[-1]))
    kv = passed_along(kv, "pipe", -1)
    got = kv[:, 2 * local:2 * local + 3, :].astype(jnp.float32)
    correction = ((got[:, 0] + got[:, 1]) + got[:, 2]).reshape(length, 1)
    slot_index, slot_valid = slot_table(random_list, global_list, head_radius, block_count)
    previous = None
    for parity in range(per_chunk):
        qd, _ = lax.optimization_barrier((shipped[parity], after))
        qd = lax.all_to_all(qd, "ctx", split_axis=0, concat_axis=0, tiled=True)
        after = qd
        result = head_part(
            kv, qd, correction, slot_index, slot_valid, previous, block_count, chunks, local,
            parity,
        )
        previous = result
    back = lax.all_to_all(result[0], "ctx", split_axis=0, concat_axis=0, tiled=True)
    outs = [back[:, k * local:(k + 1) * local] for k in range(3)]
    return tuple(o.transpose(1, 0, 2).reshape(1, local, chunks * HD) for o in outs)


def solution(mesh):
    return jax.shard_map(
        body,
        mesh=mesh,
        in_specs=(
            P("pipe", "ctx", None),
            P("pipe", "ctx", None),
            P("pipe", "ctx", None),
            P("pipe", "ctx", None),
            P("pipe", "ctx", None),
            P("pipe", "ctx", None, None),
            P("pipe", None),
            P("pipe", "ctx"),
        ),
        out_specs=(P("pipe", "ctx", None), P("pipe", "ctx", None), P("pipe", "ctx", None)),
        check_vma=False,
    )
```

```python
import functools

import jax
import jax.numpy as jnp
from jax import lax
from jax.experimental import pallas as pl
from jax.experimental.pallas import tpu as pltpu
from jax.sharding import PartitionSpec as P


HD = 128
BLK = 64
RMAX = 2
NR = 3
KB = 10


def passed_along(value, axis, steps):
    count = lax.axis_size(axis)
    pairs = [(source, (source + steps) % count) for source in range(count)]
    return lax.ppermute(value, axis, pairs)


def slot_table(random_list, global_list, head_radius, block_count):
    blocks = jnp.arange(block_count, dtype=jnp.int32)[:, None]
    offsets = jnp.arange(-RMAX, RMAX + 1, dtype=jnp.int32)[None, :]
    window = blocks + offsets
    window_ok = (jnp.abs(offsets) <= head_radius) & (window >= 0) & (window < block_count)
    window = jnp.clip(window, 0, block_count - 1)
    global_slots = jnp.broadcast_to(global_list[None, :], (block_count, global_list.shape[0]))
    global_ok = jnp.abs(global_slots - blocks) > head_radius
    random_ok = jnp.abs(random_list - blocks) > head_radius
    random_ok = random_ok & jnp.all(random_list[:, :, None] != global_list[None, None, :], axis=2)
    earlier = jnp.arange(NR)[None, :] < jnp.arange(NR)[:, None]
    repeated = jnp.any((random_list[:, :, None] == random_list[:, None, :]) & earlier[None], axis=2)
    random_ok = random_ok & jnp.logical_not(repeated)
    slot_index = jnp.concatenate([window, global_slots, random_list], axis=1)
    slot_valid = jnp.concatenate([window_ok, global_ok, random_ok], axis=1)
    slot_index = jnp.clip(slot_index, 0, block_count - 1)
    return (slot_index.astype(jnp.int32), slot_valid.astype(jnp.int32))


def head_kernel(slot_ref, valid_ref, kv_ref, qd_ref, corr_ref, *rest, block_count,
                chunk_rows, parity, final):
    if final:
        (dk_prev, dv_prev, out_ref, kt_ref, vt_ref, dk_acc, dv_acc) = rest
        dq_ref = out_ref.at[:, 0:BLK, :]
        dk_ref = out_ref.at[:, BLK:BLK + chunk_rows, :]
        dv_ref = out_ref.at[:, BLK + chunk_rows:BLK + 2 * chunk_rows, :]
    else:
        (dq_ref, dk_acc, dv_acc, kt_ref, vt_ref) = rest
    score_scale = HD ** (-0.5)
    per_chunk = chunk_rows // BLK
    dk_acc[...] = jnp.zeros_like(dk_acc)
    dv_acc[...] = jnp.zeros_like(dv_acc)
    lane_slot = lax.broadcasted_iota(jnp.int32, (1, KB * BLK), 1) // BLK

    def one_block(t, carry):
        i = t * per_chunk + parity
        query = qd_ref[t, 0]
        grad = qd_ref[t, 1]
        live = jnp.zeros((1, KB * BLK), jnp.bool_)
        for j in range(KB):
            kb = slot_ref[i * KB + j]
            kc = kb // per_chunk
            kr = pl.multiple_of((kb % per_chunk) * BLK, BLK)
            kt_ref[pl.ds(j * BLK, BLK), :] = kv_ref[kc, pl.ds(kr, BLK), :]
            vt_ref[pl.ds(j * BLK, BLK), :] = kv_ref[kc, pl.ds(chunk_rows + kr, BLK), :]
            live = live | ((lane_slot == j) & (valid_ref[i * KB + j] != 0))
        key_tiles = kt_ref[...]
        value_tiles = vt_ref[...]
        scores = lax.dot_general(
            query, key_tiles, (((1,), (1,)), ((), ())), preferred_element_type=jnp.float32
        ) * score_scale
        scores = jnp.where(live, scores, -jnp.inf)
        row_max = jnp.max(scores, axis=-1, keepdims=True)
        weights = jnp.exp(scores - row_max)
        attention = weights / jnp.sum(weights, axis=-1, keepdims=True)
        dprobs = lax.dot_general(
            grad, value_tiles, (((1,), (1,)), ((), ())), preferred_element_type=jnp.float32
        )
        corr = corr_ref[pl.ds(pl.multiple_of(i * BLK, BLK), BLK), :]
        dscores = (attention * (dprobs - corr)).astype(jnp.bfloat16)
        query_grad = jnp.dot(dscores, key_tiles, preferred_element_type=jnp.float32) * score_scale
        dq_ref[t] = query_grad.astype(jnp.bfloat16)
        key_part = lax.dot_general(
            dscores, query, (((0,), (0,)), ((), ())), preferred_element_type=jnp.float32
        )
        value_part = lax.dot_general(
            attention.astype(jnp.bfloat16), grad, (((0,), (0,)), ((), ())),
            preferred_element_type=jnp.float32,
        )
        for j in range(KB):
            kb = slot_ref[i * KB + j]
            dk_acc[kb] = dk_acc[kb] + key_part[j * BLK:(j + 1) * BLK]
            dv_acc[kb] = dv_acc[kb] + value_part[j * BLK:(j + 1) * BLK]
        return carry

    lax.fori_loop(0, block_count // per_chunk, one_block, 0)

    if final:
        def one_chunk(c, carry):
            for p in range(per_chunk):
                b = c * per_chunk + p
                dk_ref[c, p * BLK:(p + 1) * BLK, :] = (
                    (dk_acc[b] + dk_prev[b]) * score_scale
                ).astype(jnp.bfloat16)
                dv_ref[c, p * BLK:(p + 1) * BLK, :] = (dv_acc[b] + dv_prev[b]).astype(
                    jnp.bfloat16
                )
            return carry

        lax.fori_loop(0, block_count // per_chunk, one_chunk, 0)


def head_part(kv, qd, corr, slot_index, slot_valid, previous, block_count, chunks, chunk_rows,
              parity):
    vmem = pltpu.MemorySpace.VMEM
    smem = pltpu.MemorySpace.SMEM
    final = previous is not None
    dq_shape = jax.ShapeDtypeStruct((chunks, BLK, HD), jnp.bfloat16)
    acc_shape = jax.ShapeDtypeStruct((block_count, BLK, HD), jnp.float32)
    kernel = functools.partial(
        head_kernel, block_count=block_count, chunk_rows=chunk_rows, parity=parity, final=final
    )
    operands = [slot_index.reshape(-1), slot_valid.reshape(-1), kv, qd, corr]
    scratch = [pltpu.VMEM((KB * BLK, HD), jnp.bfloat16), pltpu.VMEM((KB * BLK, HD), jnp.bfloat16)]
    if final:
        operands += list(previous[1:])
        out_shape = (jax.ShapeDtypeStruct((chunks, BLK + 2 * chunk_rows, HD), jnp.bfloat16),)
        scratch += [pltpu.VMEM((block_count, BLK, HD), jnp.float32)] * 2
    else:
        out_shape = (dq_shape, acc_shape, acc_shape)
    in_specs = [pl.BlockSpec(memory_space=smem)] * 2 + [pl.BlockSpec(memory_space=vmem)] * (
        len(operands) - 2
    )
    return pl.pallas_call(
        kernel,
        out_shape=out_shape,
        in_specs=in_specs,
        out_specs=tuple(pl.BlockSpec(memory_space=vmem) for _ in out_shape),
        scratch_shapes=scratch,
        compiler_params=pltpu.CompilerParams(vmem_limit_bytes=48 * 1024 * 1024),
    )(*operands)


def assemble_kernel(first_ref, back_ref, dq_ref, dk_ref, dv_ref, *, local):
    for h in range(first_ref.shape[0]):
        cols = slice(h * HD, (h + 1) * HD)
        dq_ref[0, 0:BLK, cols] = first_ref[h]
        dq_ref[0, BLK:2 * BLK, cols] = back_ref[h, 0:BLK, :]
        dk_ref[0, :, cols] = back_ref[h, BLK:BLK + local, :]
        dv_ref[0, :, cols] = back_ref[h, BLK + local:BLK + 2 * local, :]


def assemble(first, back, local):
    vmem = pltpu.MemorySpace.VMEM
    shape = jax.ShapeDtypeStruct((1, local, first.shape[0] * HD), jnp.bfloat16)
    return pl.pallas_call(
        functools.partial(assemble_kernel, local=local),
        out_shape=(shape, shape, shape),
        in_specs=[pl.BlockSpec(memory_space=vmem)] * 2,
        out_specs=tuple(pl.BlockSpec(memory_space=vmem) for _ in range(3)),
    )(first, back)


def to_chunks(rows, chunks):
    count, local, width = rows.shape
    return rows.reshape(count, local, chunks, width // chunks).transpose(2, 0, 1, 3)


def split_pieces(value, count):
    pieces = []
    rest = value
    for _ in range(count):
        piece = lax.optimization_barrier(rest.astype(jnp.bfloat16))
        pieces.append(piece)
        rest = rest - piece.astype(jnp.float32)
    return pieces


def body(queries, keys, values, attn_out, out_grad, random_blocks, global_blocks, radius):
    chunks = lax.axis_size("ctx")
    local = queries.shape[1]
    width = queries.shape[2]
    heads = width // HD
    length = local * chunks
    block_count = length // BLK
    per_chunk = local // BLK
    ints = jnp.concatenate(
        [random_blocks.reshape(-1), global_blocks.reshape(-1), radius.reshape(-1)]
    )
    ints = passed_along(ints, "pipe", -1)
    random_list = ints[:block_count * NR].reshape(block_count, NR)
    global_list = ints[block_count * NR:-1]
    head_radius = ints[-1]
    shipped = []
    for parity in range(per_chunk):
        rows = slice(parity * BLK, (parity + 1) * BLK)
        qd = to_chunks(jnp.stack([queries[0, rows], out_grad[0, rows]], axis=0), chunks)
        qd, _ = lax.optimization_barrier((qd, ints))
        shipped.append(passed_along(qd, "pipe", -1))
    correction = jnp.sum(
        (attn_out[0].astype(jnp.float32) * out_grad[0].astype(jnp.float32)).reshape(
            local, heads, HD
        ),
        axis=-1,
    )
    pieces = jnp.stack(split_pieces(correction.T, 3), axis=1)
    pieces = jnp.pad(pieces, ((0, 0), (0, 8 - pieces.shape[1]), (0, 0)))
    kv = to_chunks(jnp.stack([keys[0], values[0]], axis=0), chunks).reshape(chunks, 2 * local, HD)
    kv = jnp.concatenate([kv, pieces], axis=1)
    kv = lax.all_to_all(kv, "ctx", split_axis=0, concat_axis=0, tiled=True)
    after = kv
    kv, _ = lax.optimization_barrier((kv, shipped[-1]))
    kv = passed_along(kv, "pipe", -1)
    got = kv[:, 2 * local:2 * local + 3, :].astype(jnp.float32)
    correction = ((got[:, 0] + got[:, 1]) + got[:, 2]).reshape(length, 1)
    slot_index, slot_valid = slot_table(random_list, global_list, head_radius, block_count)
    previous = None
    for parity in range(per_chunk):
        qd, _ = lax.optimization_barrier((shipped[parity], after))
        qd = lax.all_to_all(qd, "ctx", split_axis=0, concat_axis=0, tiled=True)
        after = qd
        result = head_part(
            kv, qd, correction, slot_index, slot_valid, previous, block_count, chunks, local,
            parity,
        )
        previous = result
        if parity == 0:
            dq_first = lax.all_to_all(result[0], "ctx", split_axis=0, concat_axis=0, tiled=True)
    back = lax.all_to_all(result[0], "ctx", split_axis=0, concat_axis=0, tiled=True)
    return assemble(dq_first, back, local)


def solution(mesh):
    return jax.shard_map(
        body,
        mesh=mesh,
        in_specs=(
            P("pipe", "ctx", None),
            P("pipe", "ctx", None),
            P("pipe", "ctx", None),
            P("pipe", "ctx", None),
            P("pipe", "ctx", None),
            P("pipe", "ctx", None, None),
            P("pipe", None),
            P("pipe", "ctx"),
        ),
        out_specs=(P("pipe", "ctx", None), P("pipe", "ctx", None), P("pipe", "ctx", None)),
        check_vma=False,
    )
```

```python
import functools

import jax
import jax.numpy as jnp
from jax import lax
from jax.experimental import pallas as pl
from jax.experimental.pallas import tpu as pltpu
from jax.sharding import PartitionSpec as P


HD = 128
BLK = 64
RMAX = 2
NR = 3
KB = 10


def passed_along(value, axis, steps):
    count = lax.axis_size(axis)
    pairs = [(source, (source + steps) % count) for source in range(count)]
    return lax.ppermute(value, axis, pairs)


def slot_table(random_list, global_list, head_radius, block_count):
    blocks = jnp.arange(block_count, dtype=jnp.int32)[:, None]
    offsets = jnp.arange(-RMAX, RMAX + 1, dtype=jnp.int32)[None, :]
    window = blocks + offsets
    window_ok = (jnp.abs(offsets) <= head_radius) & (window >= 0) & (window < block_count)
    window = jnp.clip(window, 0, block_count - 1)
    global_slots = jnp.broadcast_to(global_list[None, :], (block_count, global_list.shape[0]))
    global_ok = jnp.abs(global_slots - blocks) > head_radius
    random_ok = jnp.abs(random_list - blocks) > head_radius
    random_ok = random_ok & jnp.all(random_list[:, :, None] != global_list[None, None, :], axis=2)
    earlier = jnp.arange(NR)[None, :] < jnp.arange(NR)[:, None]
    repeated = jnp.any((random_list[:, :, None] == random_list[:, None, :]) & earlier[None], axis=2)
    random_ok = random_ok & jnp.logical_not(repeated)
    slot_index = jnp.concatenate([window, global_slots, random_list], axis=1)
    slot_valid = jnp.concatenate([window_ok, global_ok, random_ok], axis=1)
    slot_index = jnp.clip(slot_index, 0, block_count - 1)
    return (slot_index.astype(jnp.int32), slot_valid.astype(jnp.int32))


def head_kernel(slot_ref, valid_ref, kv_ref, qd_ref, corr_ref, *rest, block_count,
                chunk_rows, parity, final):
    if final:
        (dk_prev, dv_prev, out_ref, kt_ref, vt_ref, dk_acc, dv_acc) = rest
        dq_ref = out_ref.at[:, 0:BLK, :]
        dk_ref = out_ref.at[:, BLK:BLK + chunk_rows, :]
        dv_ref = out_ref.at[:, BLK + chunk_rows:BLK + 2 * chunk_rows, :]
    else:
        (dq_ref, dk_acc, dv_acc, kt_ref, vt_ref) = rest
    score_scale = HD ** (-0.5)
    per_chunk = chunk_rows // BLK
    dk_acc[...] = jnp.zeros_like(dk_acc)
    dv_acc[...] = jnp.zeros_like(dv_acc)
    lane_slot = lax.broadcasted_iota(jnp.int32, (1, KB * BLK), 1) // BLK

    def one_block(t, u):
        i = t * per_chunk + parity
        query = qd_ref[t, 0]
        grad = qd_ref[t, 1]
        live = jnp.zeros((1, KB * BLK), jnp.bool_)
        for j in range(KB):
            kb = slot_ref[i * KB + j]
            kc = kb // per_chunk
            kr = pl.multiple_of((kb % per_chunk) * BLK, BLK)
            kt_ref[u, pl.ds(j * BLK, BLK), :] = kv_ref[kc, pl.ds(kr, BLK), :]
            vt_ref[u, pl.ds(j * BLK, BLK), :] = kv_ref[kc, pl.ds(chunk_rows + kr, BLK), :]
            live = live | ((lane_slot == j) & (valid_ref[i * KB + j] != 0))
        key_tiles = kt_ref[u]
        value_tiles = vt_ref[u]
        scores = lax.dot_general(
            query, key_tiles, (((1,), (1,)), ((), ())), preferred_element_type=jnp.float32
        ) * score_scale
        scores = jnp.where(live, scores, -jnp.inf)
        row_max = jnp.max(scores, axis=-1, keepdims=True)
        weights = jnp.exp(scores - row_max)
        attention = weights / jnp.sum(weights, axis=-1, keepdims=True)
        dprobs = lax.dot_general(
            grad, value_tiles, (((1,), (1,)), ((), ())), preferred_element_type=jnp.float32
        )
        corr = corr_ref[pl.ds(pl.multiple_of(i * BLK, BLK), BLK), :]
        dscores = (attention * (dprobs - corr)).astype(jnp.bfloat16)
        query_grad = jnp.dot(dscores, key_tiles, preferred_element_type=jnp.float32) * score_scale
        dq_ref[t] = query_grad.astype(jnp.bfloat16)
        key_part = lax.dot_general(
            dscores, query, (((0,), (0,)), ((), ())), preferred_element_type=jnp.float32
        )
        value_part = lax.dot_general(
            attention.astype(jnp.bfloat16), grad, (((0,), (0,)), ((), ())),
            preferred_element_type=jnp.float32,
        )
        return i, key_part, value_part

    def scatter(i, key_part, value_part):
        for j in range(KB):
            kb = slot_ref[i * KB + j]
            dk_acc[kb] = dk_acc[kb] + key_part[j * BLK:(j + 1) * BLK]
            dv_acc[kb] = dv_acc[kb] + value_part[j * BLK:(j + 1) * BLK]

    def two_blocks(t2, carry):
        first = one_block(2 * t2, 0)
        second = one_block(2 * t2 + 1, 1)
        scatter(*first)
        scatter(*second)
        return carry

    lax.fori_loop(0, block_count // per_chunk // 2, two_blocks, 0)

    if final:
        def one_chunk(c, carry):
            for p in range(per_chunk):
                b = c * per_chunk + p
                dk_ref[c, p * BLK:(p + 1) * BLK, :] = (
                    (dk_acc[b] + dk_prev[b]) * score_scale
                ).astype(jnp.bfloat16)
                dv_ref[c, p * BLK:(p + 1) * BLK, :] = (dv_acc[b] + dv_prev[b]).astype(
                    jnp.bfloat16
                )
            return carry

        lax.fori_loop(0, block_count // per_chunk, one_chunk, 0)


def head_part(kv, qd, corr, slot_index, slot_valid, previous, block_count, chunks, chunk_rows,
              parity):
    vmem = pltpu.MemorySpace.VMEM
    smem = pltpu.MemorySpace.SMEM
    final = previous is not None
    dq_shape = jax.ShapeDtypeStruct((chunks, BLK, HD), jnp.bfloat16)
    acc_shape = jax.ShapeDtypeStruct((block_count, BLK, HD), jnp.float32)
    kernel = functools.partial(
        head_kernel, block_count=block_count, chunk_rows=chunk_rows, parity=parity, final=final
    )
    operands = [slot_index.reshape(-1), slot_valid.reshape(-1), kv, qd, corr]
    scratch = [pltpu.VMEM((2, KB * BLK, HD), jnp.bfloat16), pltpu.VMEM((2, KB * BLK, HD), jnp.bfloat16)]
    if final:
        operands += list(previous[1:])
        out_shape = (jax.ShapeDtypeStruct((chunks, BLK + 2 * chunk_rows, HD), jnp.bfloat16),)
        scratch += [pltpu.VMEM((block_count, BLK, HD), jnp.float32)] * 2
    else:
        out_shape = (dq_shape, acc_shape, acc_shape)
    in_specs = [pl.BlockSpec(memory_space=smem)] * 2 + [pl.BlockSpec(memory_space=vmem)] * (
        len(operands) - 2
    )
    return pl.pallas_call(
        kernel,
        out_shape=out_shape,
        in_specs=in_specs,
        out_specs=tuple(pl.BlockSpec(memory_space=vmem) for _ in out_shape),
        scratch_shapes=scratch,
        compiler_params=pltpu.CompilerParams(vmem_limit_bytes=48 * 1024 * 1024),
    )(*operands)


def assemble_kernel(first_ref, back_ref, dq_ref, dk_ref, dv_ref, *, local):
    for h in range(first_ref.shape[0]):
        cols = slice(h * HD, (h + 1) * HD)
        dq_ref[0, 0:BLK, cols] = first_ref[h]
        dq_ref[0, BLK:2 * BLK, cols] = back_ref[h, 0:BLK, :]
        dk_ref[0, :, cols] = back_ref[h, BLK:BLK + local, :]
        dv_ref[0, :, cols] = back_ref[h, BLK + local:BLK + 2 * local, :]


def assemble(first, back, local):
    vmem = pltpu.MemorySpace.VMEM
    shape = jax.ShapeDtypeStruct((1, local, first.shape[0] * HD), jnp.bfloat16)
    return pl.pallas_call(
        functools.partial(assemble_kernel, local=local),
        out_shape=(shape, shape, shape),
        in_specs=[pl.BlockSpec(memory_space=vmem)] * 2,
        out_specs=tuple(pl.BlockSpec(memory_space=vmem) for _ in range(3)),
    )(first, back)


def to_chunks(rows, chunks):
    count, local, width = rows.shape
    return rows.reshape(count, local, chunks, width // chunks).transpose(2, 0, 1, 3)


def split_pieces(value, count):
    pieces = []
    rest = value
    for _ in range(count):
        piece = lax.optimization_barrier(rest.astype(jnp.bfloat16))
        pieces.append(piece)
        rest = rest - piece.astype(jnp.float32)
    return pieces


def body(queries, keys, values, attn_out, out_grad, random_blocks, global_blocks, radius):
    chunks = lax.axis_size("ctx")
    local = queries.shape[1]
    width = queries.shape[2]
    heads = width // HD
    length = local * chunks
    block_count = length // BLK
    per_chunk = local // BLK
    ints = jnp.concatenate(
        [random_blocks.reshape(-1), global_blocks.reshape(-1), radius.reshape(-1)]
    )
    ints = passed_along(ints, "pipe", -1)
    random_list = ints[:block_count * NR].reshape(block_count, NR)
    global_list = ints[block_count * NR:-1]
    head_radius = ints[-1]
    shipped = []
    for parity in range(per_chunk):
        rows = slice(parity * BLK, (parity + 1) * BLK)
        qd = to_chunks(jnp.stack([queries[0, rows], out_grad[0, rows]], axis=0), chunks)
        qd, _ = lax.optimization_barrier((qd, ints))
        shipped.append(passed_along(qd, "pipe", -1))
    correction = jnp.sum(
        (attn_out[0].astype(jnp.float32) * out_grad[0].astype(jnp.float32)).reshape(
            local, heads, HD
        ),
        axis=-1,
    )
    pieces = jnp.stack(split_pieces(correction.T, 3), axis=1)
    pieces = jnp.pad(pieces, ((0, 0), (0, 8 - pieces.shape[1]), (0, 0)))
    kv = to_chunks(jnp.stack([keys[0], values[0]], axis=0), chunks).reshape(chunks, 2 * local, HD)
    kv = jnp.concatenate([kv, pieces], axis=1)
    kv = lax.all_to_all(kv, "ctx", split_axis=0, concat_axis=0, tiled=True)
    after = kv
    kv, _ = lax.optimization_barrier((kv, shipped[-1]))
    kv = passed_along(kv, "pipe", -1)
    slot_index, slot_valid = slot_table(random_list, global_list, head_radius, block_count)
    previous = None
    for parity in range(per_chunk):
        qd, _ = lax.optimization_barrier((shipped[parity], after))
        qd = lax.all_to_all(qd, "ctx", split_axis=0, concat_axis=0, tiled=True)
        after = qd
        if parity == 0:
            got = kv[:, 2 * local:2 * local + 3, :].astype(jnp.float32)
            correction = ((got[:, 0] + got[:, 1]) + got[:, 2]).reshape(length, 1)
        result = head_part(
            kv, qd, correction, slot_index, slot_valid, previous, block_count, chunks, local,
            parity,
        )
        previous = result
        if parity == 0:
            dq_first = lax.all_to_all(result[0], "ctx", split_axis=0, concat_axis=0, tiled=True)
    back = lax.all_to_all(result[0], "ctx", split_axis=0, concat_axis=0, tiled=True)
    return assemble(dq_first, back, local)


def solution(mesh):
    return jax.shard_map(
        body,
        mesh=mesh,
        in_specs=(
            P("pipe", "ctx", None),
            P("pipe", "ctx", None),
            P("pipe", "ctx", None),
            P("pipe", "ctx", None),
            P("pipe", "ctx", None),
            P("pipe", "ctx", None, None),
            P("pipe", None),
            P("pipe", "ctx"),
        ),
        out_specs=(P("pipe", "ctx", None), P("pipe", "ctx", None), P("pipe", "ctx", None)),
        check_vma=False,
    )
```

```python
import functools

import jax
import jax.numpy as jnp
from jax import lax
from jax.experimental import pallas as pl
from jax.experimental.pallas import tpu as pltpu
from jax.sharding import PartitionSpec as P


HD = 128
BLK = 64
RMAX = 2
NR = 3
KB = 10
STEP = 8


def passed_along(value, axis, steps):
    count = lax.axis_size(axis)
    pairs = [(source, (source + steps) % count) for source in range(count)]
    return lax.ppermute(value, axis, pairs)


def slot_table(random_list, global_list, head_radius, block_count):
    blocks = jnp.arange(block_count, dtype=jnp.int32)[:, None]
    offsets = jnp.arange(-RMAX, RMAX + 1, dtype=jnp.int32)[None, :]
    window = blocks + offsets
    window_ok = (jnp.abs(offsets) <= head_radius) & (window >= 0) & (window < block_count)
    window = jnp.clip(window, 0, block_count - 1)
    global_slots = jnp.broadcast_to(global_list[None, :], (block_count, global_list.shape[0]))
    global_ok = jnp.abs(global_slots - blocks) > head_radius
    random_ok = jnp.abs(random_list - blocks) > head_radius
    random_ok = random_ok & jnp.all(random_list[:, :, None] != global_list[None, None, :], axis=2)
    earlier = jnp.arange(NR)[None, :] < jnp.arange(NR)[:, None]
    repeated = jnp.any((random_list[:, :, None] == random_list[:, None, :]) & earlier[None], axis=2)
    random_ok = random_ok & jnp.logical_not(repeated)
    slot_index = jnp.concatenate([window, global_slots, random_list], axis=1)
    slot_valid = jnp.concatenate([window_ok, global_ok, random_ok], axis=1)
    slot_index = jnp.clip(slot_index, 0, block_count - 1)
    return (slot_index.astype(jnp.int32), slot_valid.astype(jnp.int32))


def head_kernel(slot_ref, valid_ref, kv_ref, qd_ref, corr_ref, *rest, block_count,
                chunk_rows, parity, final):
    if final:
        (dk_prev, dv_prev, out_ref, kt_ref, vt_ref, dk_acc, dv_acc) = rest
        dq_ref = out_ref.at[:, 0:BLK, :]
        dk_ref = out_ref.at[:, BLK:BLK + chunk_rows, :]
        dv_ref = out_ref.at[:, BLK + chunk_rows:BLK + 2 * chunk_rows, :]
    else:
        (dq_ref, dk_acc, dv_acc, kt_ref, vt_ref) = rest
    score_scale = HD ** (-0.5)
    per_chunk = chunk_rows // BLK
    dk_acc[...] = jnp.zeros_like(dk_acc)
    dv_acc[...] = jnp.zeros_like(dv_acc)
    lane_slot = lax.broadcasted_iota(jnp.int32, (1, KB * BLK), 1) // BLK

    def one_block(t, u):
        i = t * per_chunk + parity
        query = qd_ref[t, 0]
        grad = qd_ref[t, 1]
        live = jnp.zeros((1, KB * BLK), jnp.bool_)
        for j in range(KB):
            kb = slot_ref[i * KB + j]
            kc = kb // per_chunk
            kr = pl.multiple_of((kb % per_chunk) * BLK, BLK)
            kt_ref[u, pl.ds(j * BLK, BLK), :] = kv_ref[kc, pl.ds(kr, BLK), :]
            vt_ref[u, pl.ds(j * BLK, BLK), :] = kv_ref[kc, pl.ds(chunk_rows + kr, BLK), :]
            live = live | ((lane_slot == j) & (valid_ref[i * KB + j] != 0))
        key_tiles = kt_ref[u]
        value_tiles = vt_ref[u]
        scores = lax.dot_general(
            query, key_tiles, (((1,), (1,)), ((), ())), preferred_element_type=jnp.float32
        ) * score_scale
        scores = jnp.where(live, scores, -jnp.inf)
        row_max = jnp.max(scores, axis=-1, keepdims=True)
        weights = jnp.exp(scores - row_max)
        attention = weights / jnp.sum(weights, axis=-1, keepdims=True)
        dprobs = lax.dot_general(
            grad, value_tiles, (((1,), (1,)), ((), ())), preferred_element_type=jnp.float32
        )
        corr = corr_ref[pl.ds(pl.multiple_of(i * BLK, BLK), BLK), :]
        dscores = (attention * (dprobs - corr)).astype(jnp.bfloat16)
        query_grad = jnp.dot(dscores, key_tiles, preferred_element_type=jnp.float32) * score_scale
        dq_ref[t] = query_grad.astype(jnp.bfloat16)
        key_part = lax.dot_general(
            dscores, query, (((0,), (0,)), ((), ())), preferred_element_type=jnp.float32
        )
        value_part = lax.dot_general(
            attention.astype(jnp.bfloat16), grad, (((0,), (0,)), ((), ())),
            preferred_element_type=jnp.float32,
        )
        return i, key_part, value_part

    def scatter(i, key_part, value_part):
        for j in range(KB):
            kb = slot_ref[i * KB + j]
            dk_acc[kb] = dk_acc[kb] + key_part[j * BLK:(j + 1) * BLK]
            dv_acc[kb] = dv_acc[kb] + value_part[j * BLK:(j + 1) * BLK]

    def some_blocks(t, carry):
        parts = [one_block(STEP * t + u, u) for u in range(STEP)]
        for part in parts:
            scatter(*part)
        return carry

    lax.fori_loop(0, block_count // per_chunk // STEP, some_blocks, 0)

    if final:
        def one_chunk(c, carry):
            for p in range(per_chunk):
                b = c * per_chunk + p
                dk_ref[c, p * BLK:(p + 1) * BLK, :] = (
                    (dk_acc[b] + dk_prev[b]) * score_scale
                ).astype(jnp.bfloat16)
                dv_ref[c, p * BLK:(p + 1) * BLK, :] = (dv_acc[b] + dv_prev[b]).astype(
                    jnp.bfloat16
                )
            return carry

        lax.fori_loop(0, block_count // per_chunk, one_chunk, 0)


def head_part(kv, qd, corr, slot_index, slot_valid, previous, block_count, chunks, chunk_rows,
              parity):
    vmem = pltpu.MemorySpace.VMEM
    smem = pltpu.MemorySpace.SMEM
    final = previous is not None
    dq_shape = jax.ShapeDtypeStruct((chunks, BLK, HD), jnp.bfloat16)
    acc_shape = jax.ShapeDtypeStruct((block_count, BLK, HD), jnp.float32)
    kernel = functools.partial(
        head_kernel, block_count=block_count, chunk_rows=chunk_rows, parity=parity, final=final
    )
    operands = [slot_index.reshape(-1), slot_valid.reshape(-1), kv, qd, corr]
    scratch = [
        pltpu.VMEM((STEP, KB * BLK, HD), jnp.bfloat16),
        pltpu.VMEM((STEP, KB * BLK, HD), jnp.bfloat16),
    ]
    if final:
        operands += list(previous[1:])
        out_shape = (jax.ShapeDtypeStruct((chunks, BLK + 2 * chunk_rows, HD), jnp.bfloat16),)
        scratch += [pltpu.VMEM((block_count, BLK, HD), jnp.float32)] * 2
    else:
        out_shape = (dq_shape, acc_shape, acc_shape)
    in_specs = [pl.BlockSpec(memory_space=smem)] * 2 + [pl.BlockSpec(memory_space=vmem)] * (
        len(operands) - 2
    )
    return pl.pallas_call(
        kernel,
        out_shape=out_shape,
        in_specs=in_specs,
        out_specs=tuple(pl.BlockSpec(memory_space=vmem) for _ in out_shape),
        scratch_shapes=scratch,
        compiler_params=pltpu.CompilerParams(vmem_limit_bytes=48 * 1024 * 1024),
    )(*operands)


def assemble_kernel(first_ref, back_ref, dq_ref, dk_ref, dv_ref, *, local):
    for h in range(first_ref.shape[0]):
        cols = slice(h * HD, (h + 1) * HD)
        dq_ref[0, 0:BLK, cols] = first_ref[h]
        dq_ref[0, BLK:2 * BLK, cols] = back_ref[h, 0:BLK, :]
        dk_ref[0, :, cols] = back_ref[h, BLK:BLK + local, :]
        dv_ref[0, :, cols] = back_ref[h, BLK + local:BLK + 2 * local, :]


def assemble(first, back, local):
    vmem = pltpu.MemorySpace.VMEM
    shape = jax.ShapeDtypeStruct((1, local, first.shape[0] * HD), jnp.bfloat16)
    return pl.pallas_call(
        functools.partial(assemble_kernel, local=local),
        out_shape=(shape, shape, shape),
        in_specs=[pl.BlockSpec(memory_space=vmem)] * 2,
        out_specs=tuple(pl.BlockSpec(memory_space=vmem) for _ in range(3)),
    )(first, back)


def to_chunks(rows, chunks):
    count, local, width = rows.shape
    return rows.reshape(count, local, chunks, width // chunks).transpose(2, 0, 1, 3)


def split_pieces(value, count):
    pieces = []
    rest = value
    for _ in range(count):
        piece = lax.optimization_barrier(rest.astype(jnp.bfloat16))
        pieces.append(piece)
        rest = rest - piece.astype(jnp.float32)
    return pieces


def body(queries, keys, values, attn_out, out_grad, random_blocks, global_blocks, radius):
    chunks = lax.axis_size("ctx")
    local = queries.shape[1]
    width = queries.shape[2]
    heads = width // HD
    length = local * chunks
    block_count = length // BLK
    per_chunk = local // BLK
    ints = jnp.concatenate(
        [random_blocks.reshape(-1), global_blocks.reshape(-1), radius.reshape(-1)]
    )
    ints = passed_along(ints, "pipe", -1)
    random_list = ints[:block_count * NR].reshape(block_count, NR)
    global_list = ints[block_count * NR:-1]
    head_radius = ints[-1]
    shipped = []
    for parity in range(per_chunk):
        rows = slice(parity * BLK, (parity + 1) * BLK)
        qd = to_chunks(jnp.stack([queries[0, rows], out_grad[0, rows]], axis=0), chunks)
        qd, _ = lax.optimization_barrier((qd, ints))
        shipped.append(passed_along(qd, "pipe", -1))
    correction = jnp.sum(
        (attn_out[0].astype(jnp.float32) * out_grad[0].astype(jnp.float32)).reshape(
            local, heads, HD
        ),
        axis=-1,
    )
    pieces = jnp.stack(split_pieces(correction.T, 3), axis=1)
    pieces = jnp.pad(pieces, ((0, 0), (0, 8 - pieces.shape[1]), (0, 0)))
    kv = to_chunks(jnp.stack([keys[0], values[0]], axis=0), chunks).reshape(chunks, 2 * local, HD)
    kv = jnp.concatenate([kv, pieces], axis=1)
    kv = lax.all_to_all(kv, "ctx", split_axis=0, concat_axis=0, tiled=True)
    after = kv
    kv, _ = lax.optimization_barrier((kv, shipped[-1]))
    kv = passed_along(kv, "pipe", -1)
    slot_index, slot_valid = slot_table(random_list, global_list, head_radius, block_count)
    previous = None
    for parity in range(per_chunk):
        qd, _ = lax.optimization_barrier((shipped[parity], after))
        qd = lax.all_to_all(qd, "ctx", split_axis=0, concat_axis=0, tiled=True)
        after = qd
        if parity == 0:
            got = kv[:, 2 * local:2 * local + 3, :].astype(jnp.float32)
            correction = ((got[:, 0] + got[:, 1]) + got[:, 2]).reshape(length, 1)
        result = head_part(
            kv, qd, correction, slot_index, slot_valid, previous, block_count, chunks, local,
            parity,
        )
        previous = result
        if parity == 0:
            dq_first = lax.all_to_all(result[0], "ctx", split_axis=0, concat_axis=0, tiled=True)
    back = lax.all_to_all(result[0], "ctx", split_axis=0, concat_axis=0, tiled=True)
    return assemble(dq_first, back, local)


def solution(mesh):
    return jax.shard_map(
        body,
        mesh=mesh,
        in_specs=(
            P("pipe", "ctx", None),
            P("pipe", "ctx", None),
            P("pipe", "ctx", None),
            P("pipe", "ctx", None),
            P("pipe", "ctx", None),
            P("pipe", "ctx", None, None),
            P("pipe", None),
            P("pipe", "ctx"),
        ),
        out_specs=(P("pipe", "ctx", None), P("pipe", "ctx", None), P("pipe", "ctx", None)),
        check_vma=False,
    )
```

```python
import functools

import jax
import jax.numpy as jnp
from jax import lax
from jax.experimental import pallas as pl
from jax.experimental.pallas import tpu as pltpu
from jax.sharding import PartitionSpec as P


HD = 128
BLK = 64
RMAX = 2
NR = 3
KB = 10
STEP = 16


def passed_along(value, axis, steps):
    count = lax.axis_size(axis)
    pairs = [(source, (source + steps) % count) for source in range(count)]
    return lax.ppermute(value, axis, pairs)


def slot_table(random_list, global_list, head_radius, block_count):
    blocks = jnp.arange(block_count, dtype=jnp.int32)[:, None]
    offsets = jnp.arange(-RMAX, RMAX + 1, dtype=jnp.int32)[None, :]
    window = blocks + offsets
    window_ok = (jnp.abs(offsets) <= head_radius) & (window >= 0) & (window < block_count)
    window = jnp.clip(window, 0, block_count - 1)
    global_slots = jnp.broadcast_to(global_list[None, :], (block_count, global_list.shape[0]))
    global_ok = jnp.abs(global_slots - blocks) > head_radius
    random_ok = jnp.abs(random_list - blocks) > head_radius
    random_ok = random_ok & jnp.all(random_list[:, :, None] != global_list[None, None, :], axis=2)
    earlier = jnp.arange(NR)[None, :] < jnp.arange(NR)[:, None]
    repeated = jnp.any((random_list[:, :, None] == random_list[:, None, :]) & earlier[None], axis=2)
    random_ok = random_ok & jnp.logical_not(repeated)
    slot_index = jnp.concatenate([window, global_slots, random_list], axis=1)
    slot_valid = jnp.concatenate([window_ok, global_ok, random_ok], axis=1)
    slot_index = jnp.clip(slot_index, 0, block_count - 1)
    return (slot_index.astype(jnp.int32), slot_valid.astype(jnp.int32))


def head_kernel(slot_ref, valid_ref, kv_ref, qd_ref, corr_ref, *rest, block_count,
                chunk_rows, parity, final):
    if final:
        (dk_prev, dv_prev, out_ref, kt_ref, vt_ref, dk_acc, dv_acc) = rest
        dq_ref = out_ref.at[:, 0:BLK, :]
        dk_ref = out_ref.at[:, BLK:BLK + chunk_rows, :]
        dv_ref = out_ref.at[:, BLK + chunk_rows:BLK + 2 * chunk_rows, :]
    else:
        (dq_ref, dk_acc, dv_acc, kt_ref, vt_ref) = rest
    score_scale = HD ** (-0.5)
    per_chunk = chunk_rows // BLK
    dk_acc[...] = jnp.zeros_like(dk_acc)
    dv_acc[...] = jnp.zeros_like(dv_acc)
    lane_slot = lax.broadcasted_iota(jnp.int32, (1, KB * BLK), 1) // BLK

    def one_block(t, u):
        i = t * per_chunk + parity
        query = qd_ref[t, 0:BLK, :]
        grad = qd_ref[t, BLK:2 * BLK, :]
        live = jnp.zeros((1, KB * BLK), jnp.bool_)
        for j in range(KB):
            kb = slot_ref[i * KB + j]
            kc = kb // per_chunk
            kr = pl.multiple_of((kb % per_chunk) * BLK, BLK)
            kt_ref[u, pl.ds(j * BLK, BLK), :] = kv_ref[kc, pl.ds(kr, BLK), :]
            vt_ref[u, pl.ds(j * BLK, BLK), :] = kv_ref[kc, pl.ds(chunk_rows + kr, BLK), :]
            live = live | ((lane_slot == j) & (valid_ref[i * KB + j] != 0))
        key_tiles = kt_ref[u]
        value_tiles = vt_ref[u]
        scores = lax.dot_general(
            query, key_tiles, (((1,), (1,)), ((), ())), preferred_element_type=jnp.float32
        ) * score_scale
        scores = jnp.where(live, scores, -jnp.inf)
        row_max = jnp.max(scores, axis=-1, keepdims=True)
        weights = jnp.exp(scores - row_max)
        attention = weights / jnp.sum(weights, axis=-1, keepdims=True)
        dprobs = lax.dot_general(
            grad, value_tiles, (((1,), (1,)), ((), ())), preferred_element_type=jnp.float32
        )
        corr = corr_ref[pl.ds(pl.multiple_of(i * BLK, BLK), BLK), :]
        dscores = (attention * (dprobs - corr)).astype(jnp.bfloat16)
        query_grad = jnp.dot(dscores, key_tiles, preferred_element_type=jnp.float32) * score_scale
        dq_ref[t] = query_grad.astype(jnp.bfloat16)
        key_part = lax.dot_general(
            dscores, query, (((0,), (0,)), ((), ())), preferred_element_type=jnp.float32
        )
        value_part = lax.dot_general(
            attention.astype(jnp.bfloat16), grad, (((0,), (0,)), ((), ())),
            preferred_element_type=jnp.float32,
        )
        return i, key_part, value_part

    def scatter(i, key_part, value_part):
        for j in range(KB):
            kb = slot_ref[i * KB + j]
            dk_acc[kb] = dk_acc[kb] + key_part[j * BLK:(j + 1) * BLK]
            dv_acc[kb] = dv_acc[kb] + value_part[j * BLK:(j + 1) * BLK]

    def some_blocks(t, carry):
        parts = [one_block(STEP * t + u, u) for u in range(STEP)]
        for part in parts:
            scatter(*part)
        return carry

    lax.fori_loop(0, block_count // per_chunk // STEP, some_blocks, 0)

    if final:
        def one_chunk(c, carry):
            for p in range(per_chunk):
                b = c * per_chunk + p
                dk_ref[c, p * BLK:(p + 1) * BLK, :] = (
                    (dk_acc[b] + dk_prev[b]) * score_scale
                ).astype(jnp.bfloat16)
                dv_ref[c, p * BLK:(p + 1) * BLK, :] = (dv_acc[b] + dv_prev[b]).astype(
                    jnp.bfloat16
                )
            return carry

        lax.fori_loop(0, block_count // per_chunk, one_chunk, 0)


def head_part(kv, qd, corr, slot_index, slot_valid, previous, block_count, chunks, chunk_rows,
              parity):
    vmem = pltpu.MemorySpace.VMEM
    smem = pltpu.MemorySpace.SMEM
    final = previous is not None
    dq_shape = jax.ShapeDtypeStruct((chunks, BLK, HD), jnp.bfloat16)
    acc_shape = jax.ShapeDtypeStruct((block_count, BLK, HD), jnp.float32)
    kernel = functools.partial(
        head_kernel, block_count=block_count, chunk_rows=chunk_rows, parity=parity, final=final
    )
    operands = [slot_index.reshape(-1), slot_valid.reshape(-1), kv, qd, corr]
    scratch = [
        pltpu.VMEM((STEP, KB * BLK, HD), jnp.bfloat16),
        pltpu.VMEM((STEP, KB * BLK, HD), jnp.bfloat16),
    ]
    if final:
        operands += list(previous[1:])
        out_shape = (jax.ShapeDtypeStruct((chunks, BLK + 2 * chunk_rows, HD), jnp.bfloat16),)
        scratch += [pltpu.VMEM((block_count, BLK, HD), jnp.float32)] * 2
    else:
        out_shape = (dq_shape, acc_shape, acc_shape)
    in_specs = [pl.BlockSpec(memory_space=smem)] * 2 + [pl.BlockSpec(memory_space=vmem)] * (
        len(operands) - 2
    )
    return pl.pallas_call(
        kernel,
        out_shape=out_shape,
        in_specs=in_specs,
        out_specs=tuple(pl.BlockSpec(memory_space=vmem) for _ in out_shape),
        scratch_shapes=scratch,
        compiler_params=pltpu.CompilerParams(vmem_limit_bytes=48 * 1024 * 1024),
    )(*operands)


def assemble_kernel(first_ref, back_ref, dq_ref, dk_ref, dv_ref, *, local):
    for h in range(first_ref.shape[0]):
        cols = slice(h * HD, (h + 1) * HD)
        dq_ref[0, 0:BLK, cols] = first_ref[h]
        dq_ref[0, BLK:2 * BLK, cols] = back_ref[h, 0:BLK, :]
        dk_ref[0, :, cols] = back_ref[h, BLK:BLK + local, :]
        dv_ref[0, :, cols] = back_ref[h, BLK + local:BLK + 2 * local, :]


def assemble(first, back, local):
    vmem = pltpu.MemorySpace.VMEM
    shape = jax.ShapeDtypeStruct((1, local, first.shape[0] * HD), jnp.bfloat16)
    return pl.pallas_call(
        functools.partial(assemble_kernel, local=local),
        out_shape=(shape, shape, shape),
        in_specs=[pl.BlockSpec(memory_space=vmem)] * 2,
        out_specs=tuple(pl.BlockSpec(memory_space=vmem) for _ in range(3)),
    )(first, back)


def to_chunks(rows, chunks):
    count, local, width = rows.shape
    return rows.reshape(count, local, chunks, width // chunks).transpose(2, 0, 1, 3)


def split_pieces(value, count):
    pieces = []
    rest = value
    for _ in range(count):
        piece = lax.optimization_barrier(rest.astype(jnp.bfloat16))
        pieces.append(piece)
        rest = rest - piece.astype(jnp.float32)
    return pieces


def body(queries, keys, values, attn_out, out_grad, random_blocks, global_blocks, radius):
    chunks = lax.axis_size("ctx")
    local = queries.shape[1]
    width = queries.shape[2]
    heads = width // HD
    length = local * chunks
    block_count = length // BLK
    per_chunk = local // BLK
    ints = jnp.concatenate(
        [random_blocks.reshape(-1), global_blocks.reshape(-1), radius.reshape(-1)]
    )
    ints = passed_along(ints, "pipe", -1)
    random_list = ints[:block_count * NR].reshape(block_count, NR)
    global_list = ints[block_count * NR:-1]
    head_radius = ints[-1]
    correction = jnp.sum(
        (attn_out[0].astype(jnp.float32) * out_grad[0].astype(jnp.float32)).reshape(
            local, heads, HD
        ),
        axis=-1,
    )
    pieces = jnp.stack(split_pieces(correction.T, 3), axis=1)
    pieces = jnp.pad(pieces, ((0, 0), (0, 8 - pieces.shape[1]), (0, 0)))
    shipped = []
    for parity in range(per_chunk):
        rows = slice(parity * BLK, (parity + 1) * BLK)
        qd = to_chunks(jnp.stack([queries[0, rows], out_grad[0, rows]], axis=0), chunks)
        qd = qd.reshape(chunks, 2 * BLK, HD)
        if parity == 0:
            qd = jnp.concatenate([qd, pieces], axis=1)
        qd, _ = lax.optimization_barrier((qd, ints))
        shipped.append(passed_along(qd, "pipe", -1))
    kv = to_chunks(jnp.stack([keys[0], values[0]], axis=0), chunks).reshape(chunks, 2 * local, HD)
    kv = lax.all_to_all(kv, "ctx", split_axis=0, concat_axis=0, tiled=True)
    after = kv
    kv, _ = lax.optimization_barrier((kv, shipped[-1]))
    kv = passed_along(kv, "pipe", -1)
    slot_index, slot_valid = slot_table(random_list, global_list, head_radius, block_count)
    previous = None
    for parity in range(per_chunk):
        qd, _ = lax.optimization_barrier((shipped[parity], after))
        qd = lax.all_to_all(qd, "ctx", split_axis=0, concat_axis=0, tiled=True)
        after = qd
        if parity == 0:
            got = qd[:, 2 * BLK:2 * BLK + 3, :].astype(jnp.float32)
            correction = ((got[:, 0] + got[:, 1]) + got[:, 2]).reshape(length, 1)
        result = head_part(
            kv, qd, correction, slot_index, slot_valid, previous, block_count, chunks, local,
            parity,
        )
        previous = result
        if parity == 0:
            dq_first = lax.all_to_all(result[0], "ctx", split_axis=0, concat_axis=0, tiled=True)
    back = lax.all_to_all(result[0], "ctx", split_axis=0, concat_axis=0, tiled=True)
    return assemble(dq_first, back, local)


def solution(mesh):
    return jax.shard_map(
        body,
        mesh=mesh,
        in_specs=(
            P("pipe", "ctx", None),
            P("pipe", "ctx", None),
            P("pipe", "ctx", None),
            P("pipe", "ctx", None),
            P("pipe", "ctx", None),
            P("pipe", "ctx", None, None),
            P("pipe", None),
            P("pipe", "ctx"),
        ),
        out_specs=(P("pipe", "ctx", None), P("pipe", "ctx", None), P("pipe", "ctx", None)),
        check_vma=False,
    )
```

```python
import functools

import jax
import jax.numpy as jnp
from jax import lax
from jax.experimental import pallas as pl
from jax.experimental.pallas import tpu as pltpu
from jax.sharding import PartitionSpec as P


HD = 128
BLK = 64
RMAX = 2
NR = 3
KB = 10
STEP = 16


def passed_along(value, axis, steps):
    count = lax.axis_size(axis)
    pairs = [(source, (source + steps) % count) for source in range(count)]
    return lax.ppermute(value, axis, pairs)


def slot_table(random_list, global_list, head_radius, block_count):
    blocks = jnp.arange(block_count, dtype=jnp.int32)[:, None]
    offsets = jnp.arange(-RMAX, RMAX + 1, dtype=jnp.int32)[None, :]
    window = blocks + offsets
    window_ok = (jnp.abs(offsets) <= head_radius) & (window >= 0) & (window < block_count)
    window = jnp.clip(window, 0, block_count - 1)
    global_slots = jnp.broadcast_to(global_list[None, :], (block_count, global_list.shape[0]))
    global_ok = jnp.abs(global_slots - blocks) > head_radius
    random_ok = jnp.abs(random_list - blocks) > head_radius
    random_ok = random_ok & jnp.all(random_list[:, :, None] != global_list[None, None, :], axis=2)
    earlier = jnp.arange(NR)[None, :] < jnp.arange(NR)[:, None]
    repeated = jnp.any((random_list[:, :, None] == random_list[:, None, :]) & earlier[None], axis=2)
    random_ok = random_ok & jnp.logical_not(repeated)
    slot_index = jnp.concatenate([window, global_slots, random_list], axis=1)
    slot_valid = jnp.concatenate([window_ok, global_ok, random_ok], axis=1)
    slot_index = jnp.clip(slot_index, 0, block_count - 1)
    return (slot_index.astype(jnp.int32), slot_valid.astype(jnp.int32))


def head_kernel(slot_ref, valid_ref, kv_ref, qd_ref, corr_ref, *rest, block_count,
                chunk_rows, parity, final):
    if final:
        (dk_prev, dv_prev, out_ref, kt_ref, vt_ref, dk_acc, dv_acc) = rest
        dq_ref = out_ref.at[:, 0:BLK, :]
        dk_ref = out_ref.at[:, BLK:BLK + chunk_rows, :]
        dv_ref = out_ref.at[:, BLK + chunk_rows:BLK + 2 * chunk_rows, :]
    else:
        (dq_ref, dk_acc, dv_acc, kt_ref, vt_ref) = rest
    score_scale = HD ** (-0.5)
    per_chunk = chunk_rows // BLK
    dk_acc[...] = jnp.zeros_like(dk_acc)
    dv_acc[...] = jnp.zeros_like(dv_acc)
    lane_slot = lax.broadcasted_iota(jnp.int32, (1, KB * BLK), 1) // BLK

    def one_block(t, u):
        i = t * per_chunk + parity
        query = qd_ref[t, 0:BLK, :]
        grad = qd_ref[t, BLK:2 * BLK, :]
        live = jnp.zeros((1, KB * BLK), jnp.bool_)
        for j in range(KB):
            kb = slot_ref[i * KB + j]
            kc = kb // per_chunk
            kr = pl.multiple_of((kb % per_chunk) * BLK, BLK)
            kt_ref[u, pl.ds(j * BLK, BLK), :] = kv_ref[kc, pl.ds(kr, BLK), :]
            vt_ref[u, pl.ds(j * BLK, BLK), :] = kv_ref[kc, pl.ds(chunk_rows + kr, BLK), :]
            live = live | ((lane_slot == j) & (valid_ref[i * KB + j] != 0))
        key_tiles = kt_ref[u]
        value_tiles = vt_ref[u]
        scores = lax.dot_general(
            query, key_tiles, (((1,), (1,)), ((), ())), preferred_element_type=jnp.float32
        ) * score_scale
        scores = jnp.where(live, scores, -jnp.inf)
        row_max = jnp.max(scores, axis=-1, keepdims=True)
        weights = jnp.exp(scores - row_max)
        attention = weights / jnp.sum(weights, axis=-1, keepdims=True)
        dprobs = lax.dot_general(
            grad, value_tiles, (((1,), (1,)), ((), ())), preferred_element_type=jnp.float32
        )
        corr = corr_ref[pl.ds(pl.multiple_of(i * BLK, BLK), BLK), :]
        dscores = (attention * (dprobs - corr)).astype(jnp.bfloat16)
        query_grad = jnp.dot(dscores, key_tiles, preferred_element_type=jnp.float32) * score_scale
        dq_ref[t] = query_grad.astype(jnp.bfloat16)
        key_part = lax.dot_general(
            dscores, query, (((0,), (0,)), ((), ())), preferred_element_type=jnp.float32
        )
        value_part = lax.dot_general(
            attention.astype(jnp.bfloat16), grad, (((0,), (0,)), ((), ())),
            preferred_element_type=jnp.float32,
        )
        return i, key_part, value_part

    def scatter(i, key_part, value_part):
        for j in range(KB):
            kb = slot_ref[i * KB + j]
            dk_acc[kb] = dk_acc[kb] + key_part[j * BLK:(j + 1) * BLK]
            dv_acc[kb] = dv_acc[kb] + value_part[j * BLK:(j + 1) * BLK]

    def some_blocks(t, carry):
        parts = [one_block(STEP * t + u, u) for u in range(STEP)]
        for part in parts:
            scatter(*part)
        return carry

    lax.fori_loop(0, block_count // per_chunk // STEP, some_blocks, 0)

    if final:
        def one_chunk(c, carry):
            for p in range(per_chunk):
                b = c * per_chunk + p
                dk_ref[c, p * BLK:(p + 1) * BLK, :] = (
                    (dk_acc[b] + dk_prev[b]) * score_scale
                ).astype(jnp.bfloat16)
                dv_ref[c, p * BLK:(p + 1) * BLK, :] = (dv_acc[b] + dv_prev[b]).astype(
                    jnp.bfloat16
                )
            return carry

        lax.fori_loop(0, block_count // per_chunk, one_chunk, 0)


def head_part(kv, qd, corr, slot_index, slot_valid, previous, block_count, chunks, chunk_rows,
              parity):
    vmem = pltpu.MemorySpace.VMEM
    smem = pltpu.MemorySpace.SMEM
    final = previous is not None
    dq_shape = jax.ShapeDtypeStruct((chunks, BLK, HD), jnp.bfloat16)
    acc_shape = jax.ShapeDtypeStruct((block_count, BLK, HD), jnp.float32)
    kernel = functools.partial(
        head_kernel, block_count=block_count, chunk_rows=chunk_rows, parity=parity, final=final
    )
    operands = [slot_index.reshape(-1), slot_valid.reshape(-1), kv, qd, corr]
    scratch = [
        pltpu.VMEM((STEP, KB * BLK, HD), jnp.bfloat16),
        pltpu.VMEM((STEP, KB * BLK, HD), jnp.bfloat16),
    ]
    if final:
        operands += list(previous[1:])
        out_shape = (jax.ShapeDtypeStruct((chunks, BLK + 2 * chunk_rows, HD), jnp.bfloat16),)
        scratch += [pltpu.VMEM((block_count, BLK, HD), jnp.float32)] * 2
    else:
        out_shape = (dq_shape, acc_shape, acc_shape)
    in_specs = [pl.BlockSpec(memory_space=smem)] * 2 + [pl.BlockSpec(memory_space=vmem)] * (
        len(operands) - 2
    )
    return pl.pallas_call(
        kernel,
        out_shape=out_shape,
        in_specs=in_specs,
        out_specs=tuple(pl.BlockSpec(memory_space=vmem) for _ in out_shape),
        scratch_shapes=scratch,
        compiler_params=pltpu.CompilerParams(vmem_limit_bytes=48 * 1024 * 1024),
    )(*operands)


def assemble_kernel(first_ref, back_ref, dq_ref, dk_ref, dv_ref, *, local):
    for h in range(first_ref.shape[0]):
        cols = slice(h * HD, (h + 1) * HD)
        dq_ref[0, 0:BLK, cols] = first_ref[h]
        dq_ref[0, BLK:2 * BLK, cols] = back_ref[h, 0:BLK, :]
        dk_ref[0, :, cols] = back_ref[h, BLK:BLK + local, :]
        dv_ref[0, :, cols] = back_ref[h, BLK + local:BLK + 2 * local, :]


def assemble(first, back, local):
    heads = first.shape[0]
    group = 8
    shape = jax.ShapeDtypeStruct((1, local, heads * HD), jnp.bfloat16)
    out_spec = pl.BlockSpec((1, local, group * HD), lambda g: (0, 0, g))
    return pl.pallas_call(
        functools.partial(assemble_kernel, local=local),
        out_shape=(shape, shape, shape),
        grid=(heads // group,),
        in_specs=[
            pl.BlockSpec((group,) + first.shape[1:], lambda g: (g, 0, 0)),
            pl.BlockSpec((group,) + back.shape[1:], lambda g: (g, 0, 0)),
        ],
        out_specs=(out_spec, out_spec, out_spec),
    )(first, back)


def to_chunks(rows, chunks):
    count, local, width = rows.shape
    return rows.reshape(count, local, chunks, width // chunks).transpose(2, 0, 1, 3)


def split_pieces(value, count):
    pieces = []
    rest = value
    for _ in range(count):
        piece = lax.optimization_barrier(rest.astype(jnp.bfloat16))
        pieces.append(piece)
        rest = rest - piece.astype(jnp.float32)
    return pieces


def body(queries, keys, values, attn_out, out_grad, random_blocks, global_blocks, radius):
    chunks = lax.axis_size("ctx")
    local = queries.shape[1]
    width = queries.shape[2]
    heads = width // HD
    length = local * chunks
    block_count = length // BLK
    per_chunk = local // BLK
    ints = jnp.concatenate(
        [random_blocks.reshape(-1), global_blocks.reshape(-1), radius.reshape(-1)]
    )
    ints = passed_along(ints, "pipe", -1)
    random_list = ints[:block_count * NR].reshape(block_count, NR)
    global_list = ints[block_count * NR:-1]
    head_radius = ints[-1]
    correction = jnp.sum(
        (attn_out[0].astype(jnp.float32) * out_grad[0].astype(jnp.float32)).reshape(
            local, heads, HD
        ),
        axis=-1,
    )
    pieces = jnp.stack(split_pieces(correction.T, 3), axis=1)
    pieces = jnp.pad(pieces, ((0, 0), (0, 8 - pieces.shape[1]), (0, 0)))
    shipped = []
    for parity in range(per_chunk):
        rows = slice(parity * BLK, (parity + 1) * BLK)
        qd = to_chunks(jnp.stack([queries[0, rows], out_grad[0, rows]], axis=0), chunks)
        qd = qd.reshape(chunks, 2 * BLK, HD)
        if parity == 0:
            qd = jnp.concatenate([qd, pieces], axis=1)
        qd, _ = lax.optimization_barrier((qd, ints))
        shipped.append(passed_along(qd, "pipe", -1))
    kv = to_chunks(jnp.stack([keys[0], values[0]], axis=0), chunks).reshape(chunks, 2 * local, HD)
    kv = lax.all_to_all(kv, "ctx", split_axis=0, concat_axis=0, tiled=True)
    after = kv
    kv, _ = lax.optimization_barrier((kv, shipped[-1]))
    kv = passed_along(kv, "pipe", -1)
    slot_index, slot_valid = slot_table(random_list, global_list, head_radius, block_count)
    previous = None
    for parity in range(per_chunk):
        qd, _ = lax.optimization_barrier((shipped[parity], after))
        qd = lax.all_to_all(qd, "ctx", split_axis=0, concat_axis=0, tiled=True)
        after = qd
        if parity == 0:
            got = qd[:, 2 * BLK:2 * BLK + 3, :].astype(jnp.float32)
            correction = ((got[:, 0] + got[:, 1]) + got[:, 2]).reshape(length, 1)
        result = head_part(
            kv, qd, correction, slot_index, slot_valid, previous, block_count, chunks, local,
            parity,
        )
        previous = result
        if parity == 0:
            dq_first = lax.all_to_all(result[0], "ctx", split_axis=0, concat_axis=0, tiled=True)
    back = lax.all_to_all(result[0], "ctx", split_axis=0, concat_axis=0, tiled=True)
    return assemble(dq_first, back, local)


def solution(mesh):
    return jax.shard_map(
        body,
        mesh=mesh,
        in_specs=(
            P("pipe", "ctx", None),
            P("pipe", "ctx", None),
            P("pipe", "ctx", None),
            P("pipe", "ctx", None),
            P("pipe", "ctx", None),
            P("pipe", "ctx", None, None),
            P("pipe", None),
            P("pipe", "ctx"),
        ),
        out_specs=(P("pipe", "ctx", None), P("pipe", "ctx", None), P("pipe", "ctx", None)),
        check_vma=False,
    )
```
